32 devices in a mesh: expert: 4 (over y, x), dp: 8 (over z, core).
Axes of the slice: x: 2, y: 2, z: 4, core: 2. Of those that a mesh axis runs over, the one named last changes fastest.
Arguments:
- routes: int32 [4096, 2], P(('expert', 'dp')), may hold values from 0 to 1, as said below
- expert_inputs: bfloat16 [8, 4, 512, 2048], P('dp', 'expert'), may hold values from -6 to 6
- hidden_grad: bfloat16 [8, 4, 512, 2048], P('dp', 'expert'), may hold values from -6 to 6
- weight: float32 [2048, 8192], P('dp', 'expert'), may hold values from -0.125 to 0.125
- moment_one: float32 [2048, 8192], P('dp', 'expert'), may hold values from -6 to 6
- moment_two: float32 [2048, 8192], P('dp', 'expert'), may hold values from 0.5 to 4
Outputs:
- token_grad: bfloat16 [4096, 2048], P(('expert', 'dp'))
- new_weight: float32 [2048, 8192], P('dp', 'expert')
- new_first: float32 [2048, 8192], P('dp', 'expert')
- new_second: float32 [2048, 8192], P('dp', 'expert')
The draws below stay inside these ranges and needn't reach their ends.
Inputs may be any that keep to these rules, and one draw needn't show every extreme that they name: `routes`: each token names 2 different experts; the tokens of one device name one expert at most 128 times, and in every device's tokens some expert is named exactly 128 times.
All inputs are finite; a program needn't handle non-finite values.
Results may differ from the reference program's by a relative error of at most 0.0045.
The reference program's roundings to bfloat16 on the way (of `masked`, `wbf` and `expert_rows`) count: a program that leaves them out, or rounds other values in their place, can miss the bound.
Values may be sent and summed in bfloat16 or wider, within the bound.
No kernel may reach another device: no remote copies, remote signals or barrier semaphores. Data moves between devices by JAX's collectives and lax.ppermute only.
A program may use at most 128 MiB of HBM per device.

```python
import math
import jax
import jax.numpy as jnp
from jax import lax

D = 2048
TOPK = 2
TOK_DEV = 128
EXPERTS = 2
FH = 2048
CAP = 128
TOKENS = 4096
N_EXPERT = 4
N_DP = 8


def draw_routes(key, part):
    blocks = TOKENS // TOK_DEV
    keys = jax.random.split(jax.random.fold_in(key, 7), blocks)
    orders = jax.vmap(lambda one: jax.random.permutation(one, EXPERTS))(keys).astype(jnp.int32)
    position = jnp.arange(TOK_DEV * TOPK, dtype=jnp.int32) // CAP
    listed = orders[:, position]
    listed = listed.reshape(blocks, TOPK, TOK_DEV)
    return jnp.transpose(listed, (0, 2, 1)).reshape(TOKENS, TOPK).astype(jnp.int32)


def levels(rng, extent, cuts, least, high):
    gain, own = 1.0, jax.random.fold_in(rng, 6)
    for dim, blocks in cuts:
        steps = jnp.exp(jax.random.uniform(jax.random.fold_in(own, dim), (blocks,), jnp.float32, least / len(cuts), high / len(cuts)))
        gain = gain * jnp.repeat(steps, extent[dim] // blocks).reshape([-1 if axis == dim else 1 for axis in range(len(extent))])
    return gain


def normal_values(stream_key, extent, scale, bound, cuts=(), kind=jnp.bfloat16):
    array = jax.random.normal(stream_key, extent, jnp.float32) * scale
    if len(cuts) > 0:
        array = levels(stream_key, extent, cuts, -0.22, 0.18) * array
    return jnp.clip(array, min=-bound, max=bound).astype(kind)


def setup_inputs(seed: int = 0) -> dict:
    seeds = jax.random.split(jax.random.key(seed), 7)
    routes = draw_routes(jax.random.fold_in(seeds[6], 71), 0)
    expert_inputs = normal_values(seeds[1], (N_DP, N_EXPERT, N_EXPERT * CAP, D), 1.0, 6.0, ((0, 8), (1, 4)))
    hidden_grad = normal_values(seeds[2], (N_DP, N_EXPERT, N_EXPERT * CAP, FH), 1.0, 6.0, ((0, 8), (1, 4)))
    weight = normal_values(seeds[3], (D, N_EXPERT * FH), D ** -0.5, 0.125, ((0, 8), (1, 4)), jnp.float32)
    moment_one = normal_values(seeds[4], (D, N_EXPERT * FH), 1.0, 6.0, ((0, 8), (1, 4)), jnp.float32)
    moment_two = jnp.clip(jnp.exp(math.log(4.0) - 2.0794415 * jax.random.uniform(seeds[5], (D, N_EXPERT * FH), jnp.float32) ** levels(seeds[5], (D, N_EXPERT * FH), ((0, 8), (1, 4)), -0.2, 0.2)), 0.5, 4.0)
    return dict(routes=routes, expert_inputs=expert_inputs, hidden_grad=hidden_grad, weight=weight, moment_one=moment_one, moment_two=moment_two)


beta_one = 0.9
beta_two = 0.95
learn_rate = 0.003
decay = 0.1
epsilon = 1e-08
loss_scale = 64.0
bias_one = 1.0 - (0.9 ** 50) ** 2
bias_two = 1.0 - (0.95 ** 50) ** 2

def adamw(weight, moment_one, moment_two, grad):
    new_first = beta_one * moment_one + (1.0 - beta_one) * grad
    new_second = beta_two * moment_two + (1.0 - beta_two) * grad * grad
    update = new_first / bias_one / (jnp.sqrt(new_second / bias_two) + epsilon)
    new_weight = weight - learn_rate * (update + decay * weight)
    return (new_weight, new_first, new_second)

def reference(routes, expert_inputs, hidden_grad, weight, moment_one, moment_two):
    routed = routes.reshape(N_EXPERT, N_DP, TOK_DEV * TOPK)
    onehot = (routed[..., None] == jnp.arange(EXPERTS, dtype=jnp.int32)).astype(jnp.int32)
    running = jnp.cumsum(onehot, axis=2)
    slots = lax.optimization_barrier(jnp.sum((running - 1) * onehot, axis=3))
    counts = lax.optimization_barrier(jnp.sum(onehot, axis=2))
    owner_counts = counts[:, :, jnp.arange(N_EXPERT) // 2]
    owner_counts = jnp.transpose(owner_counts, (1, 2, 0))
    valid = jnp.arange(CAP, dtype=jnp.int32)[None, None, None, :] < owner_counts[..., None]
    valid = valid.reshape(N_DP, N_EXPERT, N_EXPERT * CAP)
    masked = jnp.where(valid[..., None], hidden_grad, jnp.zeros_like(hidden_grad))
    wbf = weight.astype(jnp.bfloat16)

    def per_expert(index):
        total = jnp.zeros((N_DP * N_EXPERT * CAP, D), jnp.float32)
        for half in range(2):
            column = 2 * index + half
            block = lax.dynamic_index_in_dim(masked, column, 1, keepdims=False)
            wcols = lax.dynamic_slice_in_dim(wbf, column * FH, FH, 1)
            total = total + jnp.dot(block.reshape(-1, FH), wcols.T, preferred_element_type=jnp.float32)
        return total.astype(jnp.bfloat16).reshape(N_DP, N_EXPERT * CAP, D)
    expert_rows = lax.map(per_expert, jnp.arange(EXPERTS, dtype=jnp.int32))
    source_idx = jnp.arange(N_EXPERT, dtype=jnp.int32)[:, None, None]
    dp_idx = jnp.arange(N_DP, dtype=jnp.int32)[None, :, None]
    picked = expert_rows[routed, dp_idx, source_idx * CAP + slots]
    picked = picked.reshape(N_EXPERT, N_DP, TOK_DEV, TOPK, D).astype(jnp.float32)
    token_grad = lax.optimization_barrier(jnp.sum(picked, axis=3)).astype(jnp.bfloat16).reshape(TOKENS, D)

    def grad_block(column):
        inputs = lax.dynamic_index_in_dim(expert_inputs, column, 1, keepdims=False).reshape(-1, D)
        block = lax.dynamic_index_in_dim(masked, column, 1, keepdims=False).reshape(-1, FH)
        return jnp.dot(inputs.T, block, preferred_element_type=jnp.float32)
    blocks = lax.map(grad_block, jnp.arange(N_EXPERT, dtype=jnp.int32))
    grad = jnp.transpose(blocks, (1, 0, 2)).reshape(D, N_EXPERT * FH) / loss_scale
    new_weight, new_first, new_second = adamw(weight, moment_one, moment_two, grad)
    return (token_grad, new_weight, new_first, new_second)
```

```python
import jax
import jax.numpy as jnp
from jax import lax
from jax.sharding import PartitionSpec as P

beta_one = 0.9
beta_two = 0.95
learn_rate = 0.003
decay = 0.1
epsilon = 1e-08
loss_scale = 64.0
bias_one = 1.0 - (0.9**50) ** 2
bias_two = 1.0 - (0.95**50) ** 2


def adamw(weight, moment_one, moment_two, grad):
    new_first = beta_one * moment_one + (1.0 - beta_one) * grad
    new_second = beta_two * moment_two + (1.0 - beta_two) * grad * grad
    update = new_first / bias_one / (jnp.sqrt(new_second / bias_two) + epsilon)
    new_weight = weight - learn_rate * (update + decay * weight)
    return (new_weight, new_first, new_second)


def gather_counts(counts, n_expert, me_e):
    got = [counts]
    for k in range(1, n_expert):
        got.append(lax.ppermute(counts, "expert", [(i, (i + k) % n_expert) for i in range(n_expert)]))
    stacked = jnp.stack(got)
    src = (me_e - jnp.arange(n_expert, dtype=jnp.int32)) % n_expert
    return stacked[src]


def gather_rows_relative(block, n, me):
    left = [None] * n
    right = [None] * n
    cur_r = block
    cur_l = block
    for t in range(1, n):
        cur_r = lax.ppermute(cur_r, "dp", [(p, p + 1) for p in range(t - 1, n - 1)])
        right[t] = cur_r
        cur_l = lax.ppermute(cur_l, "dp", [(p, p - 1) for p in range(1, n - t + 1)])
        left[t] = cur_l
    parts = [block]
    for r in range(1, n):
        parts.append(jnp.where(me + r < n, left[r], right[n - r]))
    return jnp.concatenate(parts, axis=0)


def reduce_scatter_rows(full, n, me, rows):
    def own_block(q):
        q = jnp.clip(q, 0, n - 1)
        return lax.dynamic_slice_in_dim(full, q * rows, rows, axis=0)

    recv_r = None
    recv_l = None
    for t in range(1, n):
        pay_r = own_block(me + n - t)
        pay_l = own_block(me - n + t)
        if recv_r is not None:
            pay_r = pay_r + recv_r.astype(jnp.float32)
            pay_l = pay_l + recv_l.astype(jnp.float32)
        recv_r = lax.ppermute(pay_r.astype(jnp.bfloat16), "dp", [(p, p + 1) for p in range(0, t)])
        recv_l = lax.ppermute(pay_l.astype(jnp.bfloat16), "dp", [(p, p - 1) for p in range(n - t, n)])
    total = own_block(me)
    if recv_r is not None:
        total = total + recv_r.astype(jnp.float32) + recv_l.astype(jnp.float32)
    return total


def shards(routes, expert_inputs, hidden_grad, weight, moment_one, moment_two):
    n_expert = lax.axis_size("expert")
    n_dp = lax.axis_size("dp")
    experts = n_expert // 2
    slot_rows = expert_inputs.shape[2]
    capacity = slot_rows // n_expert
    width = expert_inputs.shape[3]
    rows = weight.shape[0]
    tok_count = routes.shape[0]
    top_count = routes.shape[1]
    me_e = lax.axis_index("expert")
    me_p = lax.axis_index("dp")
    flat_routes = routes.reshape(-1)
    onehot = (flat_routes[:, None] == jnp.arange(experts, dtype=jnp.int32)[None, :]).astype(
        jnp.int32
    )
    running = jnp.cumsum(onehot, axis=0)
    slots = jnp.sum((running - 1) * onehot, axis=1).reshape(tok_count, top_count)
    counts = jnp.sum(onehot, axis=0)
    all_counts = gather_counts(counts, n_expert, me_e)
    my_expert = me_e // 2
    chosen = jnp.arange(experts, dtype=jnp.int32)[None, :] == my_expert
    my_counts = jnp.sum(jnp.where(chosen, all_counts, 0), axis=1)
    valid = (jnp.arange(capacity, dtype=jnp.int32)[None, :] < my_counts[:, None]).reshape(-1)
    inputs_flat = expert_inputs.reshape(slot_rows, width)
    grad_flat = hidden_grad.reshape(slot_rows, -1)
    masked = jnp.where(valid[:, None], grad_flat, jnp.zeros_like(grad_flat))
    wbf = weight.astype(jnp.bfloat16)
    w_rel = gather_rows_relative(wbf, n_dp, me_p)
    partial_rows = lax.dot_general(
        masked, w_rel, (((1,), (1,)), ((), ())), preferred_element_type=jnp.float32
    )
    sent = partial_rows.reshape(n_expert, capacity, width)
    received = lax.all_to_all(sent, "expert", split_axis=0, concat_axis=0, tiled=True)
    paired = jnp.sum(received.reshape(experts, 2, capacity, width), axis=1).astype(jnp.bfloat16)
    picked = paired[routes, slots]
    token_rel = jnp.sum(picked.astype(jnp.float32), axis=1).astype(jnp.bfloat16)
    token_grad = jnp.roll(token_rel, me_p * rows, axis=1)
    full = lax.dot_general(
        inputs_flat, masked, (((0,), (0,)), ((), ())), preferred_element_type=jnp.float32
    )
    owned = reduce_scatter_rows(full, n_dp, me_p, rows)
    new_weight, new_first, new_second = adamw(weight, moment_one, moment_two, owned / loss_scale)
    return (token_grad, new_weight, new_first, new_second)


def solution(mesh):
    in_specs = (
        P(("expert", "dp"), None),
        P("dp", "expert", None, None),
        P("dp", "expert", None, None),
        P("dp", "expert"),
        P("dp", "expert"),
        P("dp", "expert"),
    )
    out_specs = (P(("expert", "dp"), None), P("dp", "expert"), P("dp", "expert"), P("dp", "expert"))
    return jax.shard_map(shards, mesh=mesh, in_specs=in_specs, out_specs=out_specs, check_vma=False)
```

```python
import jax
import jax.numpy as jnp
from jax import lax
from jax.sharding import Mesh
from jax.sharding import PartitionSpec as P

beta_one = 0.9
beta_two = 0.95
learn_rate = 0.003
decay = 0.1
epsilon = 1e-08
loss_scale = 64.0
bias_one = 1.0 - (0.9**50) ** 2
bias_two = 1.0 - (0.95**50) ** 2
CORES = 2
DP = ("z", "core")


def adamw(weight, moment_one, moment_two, grad):
    new_first = beta_one * moment_one + (1.0 - beta_one) * grad
    new_second = beta_two * moment_two + (1.0 - beta_two) * grad * grad
    update = new_first / bias_one / (jnp.sqrt(new_second / bias_two) + epsilon)
    new_weight = weight - learn_rate * (update + decay * weight)
    return (new_weight, new_first, new_second)


SWAP = [(0, 1), (1, 0)]


def shards(routes, expert_inputs, hidden_grad, weight, moment_one, moment_two):
    n_expert = lax.axis_size("expert")
    n_z = lax.axis_size("z")
    experts = n_expert // 2
    slot_rows = expert_inputs.shape[2]
    capacity = slot_rows // n_expert
    width = expert_inputs.shape[3]
    rows = weight.shape[0]
    tok_count = routes.shape[0]
    top_count = routes.shape[1]
    me_c = lax.axis_index("core")
    flat_routes = routes.reshape(-1)
    onehot = (flat_routes[:, None] == jnp.arange(experts, dtype=jnp.int32)[None, :]).astype(
        jnp.int32
    )
    running = jnp.cumsum(onehot, axis=0)
    slots = jnp.sum((running - 1) * onehot, axis=1).reshape(tok_count, top_count)
    counts = jnp.sum(onehot, axis=0)
    all_counts = lax.all_gather(counts[None, :], "expert", axis=0, tiled=True)
    my_expert = lax.axis_index("expert") // 2
    chosen = jnp.arange(experts, dtype=jnp.int32)[None, :] == my_expert
    my_counts = jnp.sum(jnp.where(chosen, all_counts, 0), axis=1)
    valid = (jnp.arange(capacity, dtype=jnp.int32)[None, :] < my_counts[:, None]).reshape(-1)
    inputs_flat = expert_inputs.reshape(slot_rows, width)
    grad_flat = hidden_grad.reshape(slot_rows, -1)
    masked = jnp.where(valid[:, None], grad_flat, jnp.zeros_like(grad_flat))

    wbf = weight.astype(jnp.bfloat16)
    w_mine = lax.all_gather(wbf, "z", axis=0, tiled=True)
    w_other = lax.ppermute(w_mine, "core", SWAP)
    w_rel = jnp.concatenate([w_mine, w_other], axis=0)
    partial_rows = lax.dot_general(
        masked, w_rel, (((1,), (1,)), ((), ())), preferred_element_type=jnp.float32
    )
    sent = partial_rows.reshape(n_expert, capacity, width)
    received = lax.all_to_all(sent, "expert", split_axis=0, concat_axis=0, tiled=True)
    paired = jnp.sum(received.reshape(experts, 2, capacity, width), axis=1).astype(jnp.bfloat16)
    picked = paired[routes, slots]
    token_rel = jnp.sum(picked.astype(jnp.float32), axis=1).astype(jnp.bfloat16)
    split = token_rel.reshape(tok_count, CORES, n_z, rows)
    split = jnp.where(me_c == 0, split, split[:, ::-1])
    token_grad = jnp.transpose(split, (0, 2, 1, 3)).reshape(tok_count, width)

    by_class = inputs_flat.reshape(slot_rows, n_z, CORES, rows)
    in_mine = lax.dynamic_index_in_dim(by_class, me_c, axis=2, keepdims=False)
    in_other = lax.dynamic_index_in_dim(by_class, 1 - me_c, axis=2, keepdims=False)
    dims = (((0,), (0,)), ((), ()))
    g_other = lax.dot_general(
        in_other.reshape(slot_rows, n_z * rows), masked, dims, preferred_element_type=jnp.float32
    )
    g_recv = lax.ppermute(g_other.astype(jnp.bfloat16), "core", SWAP)
    g_mine = lax.dot_general(
        in_mine.reshape(slot_rows, n_z * rows), masked, dims, preferred_element_type=jnp.float32
    )
    chip = (g_mine + g_recv.astype(jnp.float32)).astype(jnp.bfloat16)
    owned = lax.psum_scatter(chip, "z", scatter_dimension=0, tiled=True).astype(jnp.float32)
    new_weight, new_first, new_second = adamw(weight, moment_one, moment_two, owned / loss_scale)
    return (token_grad, new_weight, new_first, new_second)


def solution(mesh):
    n_expert, n_dp = mesh.devices.shape
    split_mesh = Mesh(mesh.devices.reshape(n_expert, n_dp // CORES, CORES), ("expert",) + DP)
    in_specs = (
        P(("expert",) + DP, None),
        P(DP, "expert", None, None),
        P(DP, "expert", None, None),
        P(DP, "expert"),
        P(DP, "expert"),
        P(DP, "expert"),
    )
    out_specs = (P(("expert",) + DP, None), P(DP, "expert"), P(DP, "expert"), P(DP, "expert"))
    return jax.shard_map(
        shards, mesh=split_mesh, in_specs=in_specs, out_specs=out_specs, check_vma=False
    )
```

```python
import jax
import jax.numpy as jnp
from jax import lax
from jax.sharding import Mesh
from jax.sharding import PartitionSpec as P

beta_one = 0.9
beta_two = 0.95
learn_rate = 0.003
decay = 0.1
epsilon = 1e-08
loss_scale = 64.0
bias_one = 1.0 - (0.9**50) ** 2
bias_two = 1.0 - (0.95**50) ** 2
CORES = 2
DP = ("z", "core")


def adamw(weight, moment_one, moment_two, grad):
    new_first = beta_one * moment_one + (1.0 - beta_one) * grad
    new_second = beta_two * moment_two + (1.0 - beta_two) * grad * grad
    update = new_first / bias_one / (jnp.sqrt(new_second / bias_two) + epsilon)
    new_weight = weight - learn_rate * (update + decay * weight)
    return (new_weight, new_first, new_second)


SWAP = [(0, 1), (1, 0)]


def gather_relative(block, axis, n, me):
    left = [None] * n
    right = [None] * n
    cur_r = block
    cur_l = block
    for t in range(1, n):
        cur_r = lax.ppermute(cur_r, axis, [(p, p + 1) for p in range(t - 1, n - 1)])
        right[t] = cur_r
        cur_l = lax.ppermute(cur_l, axis, [(p, p - 1) for p in range(1, n - t + 1)])
        left[t] = cur_l
    parts = [block]
    for r in range(1, n):
        parts.append(jnp.where(me + r < n, left[r], right[n - r]))
    return jnp.concatenate(parts, axis=0)


def shards(routes, expert_inputs, hidden_grad, weight, moment_one, moment_two):
    n_expert = lax.axis_size("expert")
    n_z = lax.axis_size("z")
    experts = n_expert // 2
    slot_rows = expert_inputs.shape[2]
    capacity = slot_rows // n_expert
    width = expert_inputs.shape[3]
    rows = weight.shape[0]
    tok_count = routes.shape[0]
    top_count = routes.shape[1]
    me_c = lax.axis_index("core")
    me_z = lax.axis_index("z")
    flat_routes = routes.reshape(-1)
    onehot = (flat_routes[:, None] == jnp.arange(experts, dtype=jnp.int32)[None, :]).astype(
        jnp.int32
    )
    running = jnp.cumsum(onehot, axis=0)
    slots = jnp.sum((running - 1) * onehot, axis=1).reshape(tok_count, top_count)
    counts = jnp.sum(onehot, axis=0)
    all_counts = lax.all_gather(counts[None, :], "expert", axis=0, tiled=True)
    my_expert = lax.axis_index("expert") // 2
    chosen = jnp.arange(experts, dtype=jnp.int32)[None, :] == my_expert
    my_counts = jnp.sum(jnp.where(chosen, all_counts, 0), axis=1)
    valid = (jnp.arange(capacity, dtype=jnp.int32)[None, :] < my_counts[:, None]).reshape(-1)
    inputs_flat = expert_inputs.reshape(slot_rows, width)
    grad_flat = hidden_grad.reshape(slot_rows, -1)
    masked = jnp.where(valid[:, None], grad_flat, jnp.zeros_like(grad_flat))

    wbf = weight.astype(jnp.bfloat16)
    w_mine = gather_relative(wbf, "z", n_z, me_z)
    w_other = lax.ppermute(w_mine, "core", SWAP)
    cols = (((1,), (1,)), ((), ()))
    out_mine = lax.dot_general(masked, w_mine, cols, preferred_element_type=jnp.float32)
    out_other = lax.dot_general(masked, w_other, cols, preferred_element_type=jnp.float32)
    partial_rows = jnp.concatenate([out_mine, out_other], axis=1)
    sent = partial_rows.reshape(n_expert, capacity, width)
    received = lax.all_to_all(sent, "expert", split_axis=0, concat_axis=0, tiled=True)
    paired = jnp.sum(received.reshape(experts, 2, capacity, width), axis=1).astype(jnp.bfloat16)
    picked = paired[routes, slots]
    token_rel = jnp.sum(picked.astype(jnp.float32), axis=1).astype(jnp.bfloat16)
    split = jnp.roll(token_rel.reshape(tok_count, CORES, n_z, rows), me_z, axis=2)
    split = jnp.where(me_c == 0, split, split[:, ::-1])
    token_grad = jnp.transpose(split, (0, 2, 1, 3)).reshape(tok_count, width)

    by_class = inputs_flat.reshape(slot_rows, n_z, CORES, rows)
    in_mine = lax.dynamic_index_in_dim(by_class, me_c, axis=2, keepdims=False)
    in_other = lax.dynamic_index_in_dim(by_class, 1 - me_c, axis=2, keepdims=False)
    dims = (((0,), (0,)), ((), ()))
    g_other = lax.dot_general(
        in_other.reshape(slot_rows, n_z * rows), masked, dims, preferred_element_type=jnp.float32
    )
    g_recv = lax.ppermute(g_other.astype(jnp.bfloat16), "core", SWAP)
    g_mine = lax.dot_general(
        in_mine.reshape(slot_rows, n_z * rows), masked, dims, preferred_element_type=jnp.float32
    )
    chip = (g_mine + g_recv.astype(jnp.float32)).astype(jnp.bfloat16)
    owned = lax.psum_scatter(chip, "z", scatter_dimension=0, tiled=True).astype(jnp.float32)
    new_weight, new_first, new_second = adamw(weight, moment_one, moment_two, owned / loss_scale)
    return (token_grad, new_weight, new_first, new_second)


def solution(mesh):
    n_expert, n_dp = mesh.devices.shape
    split_mesh = Mesh(mesh.devices.reshape(n_expert, n_dp // CORES, CORES), ("expert",) + DP)
    in_specs = (
        P(("expert",) + DP, None),
        P(DP, "expert", None, None),
        P(DP, "expert", None, None),
        P(DP, "expert"),
        P(DP, "expert"),
        P(DP, "expert"),
    )
    out_specs = (P(("expert",) + DP, None), P(DP, "expert"), P(DP, "expert"), P(DP, "expert"))
    return jax.shard_map(
        shards, mesh=split_mesh, in_specs=in_specs, out_specs=out_specs, check_vma=False
    )
```

```python
import jax
import jax.numpy as jnp
from jax import lax
from jax.sharding import Mesh
from jax.sharding import PartitionSpec as P

beta_one = 0.9
beta_two = 0.95
learn_rate = 0.003
decay = 0.1
epsilon = 1e-08
loss_scale = 64.0
bias_one = 1.0 - (0.9**50) ** 2
bias_two = 1.0 - (0.95**50) ** 2
CORES = 2
DP = ("z", "core")


def adamw(weight, moment_one, moment_two, grad):
    new_first = beta_one * moment_one + (1.0 - beta_one) * grad
    new_second = beta_two * moment_two + (1.0 - beta_two) * grad * grad
    update = new_first / bias_one / (jnp.sqrt(new_second / bias_two) + epsilon)
    new_weight = weight - learn_rate * (update + decay * weight)
    return (new_weight, new_first, new_second)


SWAP = [(0, 1), (1, 0)]


def gather_relative(block, axis, n, me):
    left = [None] * n
    right = [None] * n
    cur_r = block
    cur_l = block
    for t in range(1, n):
        cur_r = lax.ppermute(cur_r, axis, [(p, p + 1) for p in range(t - 1, n - 1)])
        right[t] = cur_r
        cur_l = lax.ppermute(cur_l, axis, [(p, p - 1) for p in range(1, n - t + 1)])
        left[t] = cur_l
    parts = [block]
    for r in range(1, n):
        parts.append(jnp.where(me + r < n, left[r], right[n - r]))
    return jnp.concatenate(parts, axis=0)


def shards(routes, expert_inputs, hidden_grad, weight, moment_one, moment_two):
    n_expert = lax.axis_size("expert")
    n_z = lax.axis_size("z")
    experts = n_expert // 2
    slot_rows = expert_inputs.shape[2]
    capacity = slot_rows // n_expert
    width = expert_inputs.shape[3]
    rows = weight.shape[0]
    tok_count = routes.shape[0]
    top_count = routes.shape[1]
    me_c = lax.axis_index("core")
    me_z = lax.axis_index("z")
    flat_routes = routes.reshape(-1)
    onehot = (flat_routes[:, None] == jnp.arange(experts, dtype=jnp.int32)[None, :]).astype(
        jnp.int32
    )
    running = jnp.cumsum(onehot, axis=0)
    slots = jnp.sum((running - 1) * onehot, axis=1).reshape(tok_count, top_count)
    counts = jnp.sum(onehot, axis=0)
    all_counts = lax.all_gather(counts[None, :], "expert", axis=0, tiled=True)
    my_expert = lax.axis_index("expert") // 2
    chosen = jnp.arange(experts, dtype=jnp.int32)[None, :] == my_expert
    my_counts = jnp.sum(jnp.where(chosen, all_counts, 0), axis=1)
    valid = (jnp.arange(capacity, dtype=jnp.int32)[None, :] < my_counts[:, None]).reshape(-1)
    inputs_flat = expert_inputs.reshape(slot_rows, width)
    grad_flat = hidden_grad.reshape(slot_rows, -1)
    masked = jnp.where(valid[:, None], grad_flat, jnp.zeros_like(grad_flat))

    wbf = weight.astype(jnp.bfloat16)
    w_mine = gather_relative(wbf, "z", n_z, me_z)
    w_other = lax.ppermute(w_mine, "core", SWAP)
    cols = (((1,), (1,)), ((), ()))
    out_mine = lax.dot_general(masked, w_mine, cols, preferred_element_type=jnp.float32)
    out_other = lax.dot_general(masked, w_other, cols, preferred_element_type=jnp.float32)
    partial_rows = jnp.concatenate([out_mine, out_other], axis=1)
    sent = partial_rows.reshape(n_expert, capacity, width)
    received = lax.all_to_all(sent, "expert", split_axis=0, concat_axis=0, tiled=True)
    paired = jnp.sum(received.reshape(experts, 2, capacity, width), axis=1).astype(jnp.bfloat16)
    picked = paired[routes, slots]
    token_rel = jnp.sum(picked.astype(jnp.float32), axis=1).astype(jnp.bfloat16)
    split = jnp.roll(token_rel.reshape(tok_count, CORES, n_z, rows), me_z, axis=2)
    split = jnp.where(me_c == 0, split, split[:, ::-1])
    token_grad = jnp.transpose(split, (0, 2, 1, 3)).reshape(tok_count, width)

    by_class = inputs_flat.reshape(slot_rows, n_z, CORES, rows)
    in_mine = lax.dynamic_index_in_dim(by_class, me_c, axis=2, keepdims=False)
    in_other = lax.dynamic_index_in_dim(by_class, 1 - me_c, axis=2, keepdims=False)
    dims = (((0,), (0,)), ((), ()))
    g_other = lax.dot_general(
        in_other.reshape(slot_rows, n_z * rows), masked, dims, preferred_element_type=jnp.float32
    )
    g_recv = lax.ppermute(g_other.astype(jnp.bfloat16), "core", SWAP)
    g_mine = lax.dot_general(
        in_mine.reshape(slot_rows, n_z * rows), masked, dims, preferred_element_type=jnp.float32
    )
    chip = (g_mine + g_recv.astype(jnp.float32)).astype(jnp.bfloat16)
    owned = lax.psum_scatter(chip, "z", scatter_dimension=0, tiled=True)
    token_grad, owned = lax.optimization_barrier((token_grad, owned))
    owned = owned.astype(jnp.float32)
    new_weight, new_first, new_second = adamw(weight, moment_one, moment_two, owned / loss_scale)
    return (token_grad, new_weight, new_first, new_second)


def solution(mesh):
    n_expert, n_dp = mesh.devices.shape
    split_mesh = Mesh(mesh.devices.reshape(n_expert, n_dp // CORES, CORES), ("expert",) + DP)
    in_specs = (
        P(("expert",) + DP, None),
        P(DP, "expert", None, None),
        P(DP, "expert", None, None),
        P(DP, "expert"),
        P(DP, "expert"),
        P(DP, "expert"),
    )
    out_specs = (P(("expert",) + DP, None), P(DP, "expert"), P(DP, "expert"), P(DP, "expert"))
    return jax.shard_map(
        shards, mesh=split_mesh, in_specs=in_specs, out_specs=out_specs, check_vma=False
    )
```

```python
import jax
import jax.numpy as jnp
from jax import lax
from jax.sharding import Mesh
from jax.sharding import PartitionSpec as P

beta_one = 0.9
beta_two = 0.95
learn_rate = 0.003
decay = 0.1
epsilon = 1e-08
loss_scale = 64.0
bias_one = 1.0 - (0.9**50) ** 2
bias_two = 1.0 - (0.95**50) ** 2
CORES = 2
DP = ("z", "core")


def adamw(weight, moment_one, moment_two, grad):
    new_first = beta_one * moment_one + (1.0 - beta_one) * grad
    new_second = beta_two * moment_two + (1.0 - beta_two) * grad * grad
    update = new_first / bias_one / (jnp.sqrt(new_second / bias_two) + epsilon)
    new_weight = weight - learn_rate * (update + decay * weight)
    return (new_weight, new_first, new_second)


SWAP = [(0, 1), (1, 0)]


def flood_first(block, axis, n):
    right = lax.ppermute(block, axis, [(p, p + 1) for p in range(0, n - 1)])
    left = lax.ppermute(block, axis, [(p, p - 1) for p in range(1, n)])
    return right, left


def gather_relative(block, first, axis, n, me):
    left = [None] * n
    right = [None] * n
    cur_r, cur_l = first
    right[1] = cur_r
    left[1] = cur_l
    for t in range(2, n):
        cur_r = lax.ppermute(cur_r, axis, [(p, p + 1) for p in range(t - 1, n - 1)])
        right[t] = cur_r
        cur_l = lax.ppermute(cur_l, axis, [(p, p - 1) for p in range(1, n - t + 1)])
        left[t] = cur_l
    parts = [block]
    for r in range(1, n):
        parts.append(jnp.where(me + r < n, left[r], right[n - r]))
    return jnp.concatenate(parts, axis=0)


def shards(routes, expert_inputs, hidden_grad, weight, moment_one, moment_two):
    n_expert = lax.axis_size("expert")
    n_z = lax.axis_size("z")
    experts = n_expert // 2
    slot_rows = expert_inputs.shape[2]
    capacity = slot_rows // n_expert
    width = expert_inputs.shape[3]
    rows = weight.shape[0]
    tok_count = routes.shape[0]
    top_count = routes.shape[1]
    me_c = lax.axis_index("core")
    me_z = lax.axis_index("z")
    wbf = weight.astype(jnp.bfloat16)
    first = flood_first(wbf, "z", n_z)
    first, routes, expert_inputs, hidden_grad = lax.optimization_barrier(
        (first, routes, expert_inputs, hidden_grad)
    )
    flat_routes = routes.reshape(-1)
    onehot = (flat_routes[:, None] == jnp.arange(experts, dtype=jnp.int32)[None, :]).astype(
        jnp.int32
    )
    running = jnp.cumsum(onehot, axis=0)
    slots = jnp.sum((running - 1) * onehot, axis=1).reshape(tok_count, top_count)
    counts = jnp.sum(onehot, axis=0)
    all_counts = lax.all_gather(counts[None, :], "expert", axis=0, tiled=True)
    my_expert = lax.axis_index("expert") // 2
    chosen = jnp.arange(experts, dtype=jnp.int32)[None, :] == my_expert
    my_counts = jnp.sum(jnp.where(chosen, all_counts, 0), axis=1)
    valid = (jnp.arange(capacity, dtype=jnp.int32)[None, :] < my_counts[:, None]).reshape(-1)
    inputs_flat = expert_inputs.reshape(slot_rows, width)
    grad_flat = hidden_grad.reshape(slot_rows, -1)
    masked = jnp.where(valid[:, None], grad_flat, jnp.zeros_like(grad_flat))

    w_mine = gather_relative(wbf, first, "z", n_z, me_z)
    w_other = lax.ppermute(w_mine, "core", SWAP)
    cols = (((1,), (1,)), ((), ()))
    half = width // CORES
    out_mine = lax.dot_general(masked, w_mine, cols, preferred_element_type=jnp.float32)
    recv_mine = lax.all_to_all(
        out_mine.reshape(n_expert, capacity, half), "expert", split_axis=0, concat_axis=0, tiled=True
    )
    out_other = lax.dot_general(masked, w_other, cols, preferred_element_type=jnp.float32)
    recv_other = lax.all_to_all(
        out_other.reshape(n_expert, capacity, half), "expert", split_axis=0, concat_axis=0, tiled=True
    )
    received = jnp.concatenate([recv_mine, recv_other], axis=2)
    paired = jnp.sum(received.reshape(experts, 2, capacity, width), axis=1).astype(jnp.bfloat16)
    picked = paired[routes, slots]
    token_rel = jnp.sum(picked.astype(jnp.float32), axis=1).astype(jnp.bfloat16)
    split = jnp.roll(token_rel.reshape(tok_count, CORES, n_z, rows), me_z, axis=2)
    split = jnp.where(me_c == 0, split, split[:, ::-1])
    token_grad = jnp.transpose(split, (0, 2, 1, 3)).reshape(tok_count, width)

    by_class = inputs_flat.reshape(slot_rows, n_z, CORES, rows)
    in_mine = lax.dynamic_index_in_dim(by_class, me_c, axis=2, keepdims=False)
    in_other = lax.dynamic_index_in_dim(by_class, 1 - me_c, axis=2, keepdims=False)
    dims = (((0,), (0,)), ((), ()))
    g_other = lax.dot_general(
        in_other.reshape(slot_rows, n_z * rows), masked, dims, preferred_element_type=jnp.float32
    )
    g_recv = lax.ppermute(g_other.astype(jnp.bfloat16), "core", SWAP)
    g_mine = lax.dot_general(
        in_mine.reshape(slot_rows, n_z * rows), masked, dims, preferred_element_type=jnp.float32
    )
    chip = (g_mine + g_recv.astype(jnp.float32)).astype(jnp.bfloat16)
    owned = lax.psum_scatter(chip, "z", scatter_dimension=0, tiled=True)
    token_grad, owned = lax.optimization_barrier((token_grad, owned))
    owned = owned.astype(jnp.float32)
    new_weight, new_first, new_second = adamw(weight, moment_one, moment_two, owned / loss_scale)
    return (token_grad, new_weight, new_first, new_second)


def solution(mesh):
    n_expert, n_dp = mesh.devices.shape
    split_mesh = Mesh(mesh.devices.reshape(n_expert, n_dp // CORES, CORES), ("expert",) + DP)
    in_specs = (
        P(("expert",) + DP, None),
        P(DP, "expert", None, None),
        P(DP, "expert", None, None),
        P(DP, "expert"),
        P(DP, "expert"),
        P(DP, "expert"),
    )
    out_specs = (P(("expert",) + DP, None), P(DP, "expert"), P(DP, "expert"), P(DP, "expert"))
    return jax.shard_map(
        shards, mesh=split_mesh, in_specs=in_specs, out_specs=out_specs, check_vma=False
    )
```

```python
import jax
import jax.numpy as jnp
from jax import lax
from jax.sharding import Mesh
from jax.sharding import PartitionSpec as P

beta_one = 0.9
beta_two = 0.95
learn_rate = 0.003
decay = 0.1
epsilon = 1e-08
loss_scale = 64.0
bias_one = 1.0 - (0.9**50) ** 2
bias_two = 1.0 - (0.95**50) ** 2
CORES = 2
DP = ("z", "core")


def adamw(weight, moment_one, moment_two, grad):
    new_first = beta_one * moment_one + (1.0 - beta_one) * grad
    new_second = beta_two * moment_two + (1.0 - beta_two) * grad * grad
    update = new_first / bias_one / (jnp.sqrt(new_second / bias_two) + epsilon)
    new_weight = weight - learn_rate * (update + decay * weight)
    return (new_weight, new_first, new_second)


SWAP = [(0, 1), (1, 0)]


def ring_order(n_z):
    count = CORES * n_z
    pos_of = [z if c == 0 else count - 1 - z for z in range(n_z) for c in range(CORES)]
    at_pos = [0] * count
    for p, j in enumerate(pos_of):
        at_pos[j] = p
    pairs = [(at_pos[j], at_pos[(j + 1) % count]) for j in range(count)]
    return pos_of, pairs


def shards(routes, expert_inputs, hidden_grad, weight, moment_one, moment_two):
    n_expert = lax.axis_size("expert")
    n_z = lax.axis_size("z")
    experts = n_expert // 2
    slot_rows = expert_inputs.shape[2]
    capacity = slot_rows // n_expert
    width = expert_inputs.shape[3]
    rows = weight.shape[0]
    tok_count = routes.shape[0]
    top_count = routes.shape[1]
    me_c = lax.axis_index("core")
    me_z = lax.axis_index("z")
    flat_routes = routes.reshape(-1)
    onehot = (flat_routes[:, None] == jnp.arange(experts, dtype=jnp.int32)[None, :]).astype(
        jnp.int32
    )
    running = jnp.cumsum(onehot, axis=0)
    slots = jnp.sum((running - 1) * onehot, axis=1).reshape(tok_count, top_count)
    counts = jnp.sum(onehot, axis=0)
    all_counts = lax.all_gather(counts[None, :], "expert", axis=0, tiled=True)
    my_expert = lax.axis_index("expert") // 2
    chosen = jnp.arange(experts, dtype=jnp.int32)[None, :] == my_expert
    my_counts = jnp.sum(jnp.where(chosen, all_counts, 0), axis=1)
    valid = (jnp.arange(capacity, dtype=jnp.int32)[None, :] < my_counts[:, None]).reshape(-1)
    inputs_flat = expert_inputs.reshape(slot_rows, width)
    grad_flat = hidden_grad.reshape(slot_rows, -1)
    masked = jnp.where(valid[:, None], grad_flat, jnp.zeros_like(grad_flat))

    pos_of, pairs = ring_order(n_z)
    count = CORES * n_z
    me_pos = jnp.asarray(pos_of, jnp.int32)[me_z * CORES + me_c]
    wbf = weight.astype(jnp.bfloat16)
    cols = (((1,), (1,)), ((), ()))
    cur = wbf
    held = [wbf]
    recv = []
    for t in range(1, count):
        cur = lax.ppermute(cur, DP, pairs)
        held.append(cur)
        if t % 2 == 1:
            w_pair = jnp.concatenate(held[t - 1 : t + 1], axis=0)
            out = lax.dot_general(masked, w_pair, cols, preferred_element_type=jnp.float32)
            recv.append(
                lax.all_to_all(
                    out.reshape(n_expert, capacity, 2 * rows),
                    "expert",
                    split_axis=0,
                    concat_axis=0,
                    tiled=True,
                )
            )
    received = jnp.concatenate(recv, axis=2)
    paired = jnp.sum(received.reshape(experts, 2, capacity, width), axis=1).astype(jnp.bfloat16)
    picked = paired[routes, slots]
    token_step = jnp.sum(picked.astype(jnp.float32), axis=1).astype(jnp.bfloat16)
    step_of = (me_pos - jnp.asarray(pos_of, jnp.int32)) % count
    token_grad = jnp.take(token_step.reshape(tok_count, count, rows), step_of, axis=1)
    token_grad = token_grad.reshape(tok_count, width)

    by_class = inputs_flat.reshape(slot_rows, n_z, CORES, rows)
    in_mine = lax.dynamic_index_in_dim(by_class, me_c, axis=2, keepdims=False)
    in_other = lax.dynamic_index_in_dim(by_class, 1 - me_c, axis=2, keepdims=False)
    dims = (((0,), (0,)), ((), ()))
    g_other = lax.dot_general(
        in_other.reshape(slot_rows, n_z * rows), masked, dims, preferred_element_type=jnp.float32
    )
    g_recv = lax.ppermute(g_other.astype(jnp.bfloat16), "core", SWAP)
    g_mine = lax.dot_general(
        in_mine.reshape(slot_rows, n_z * rows), masked, dims, preferred_element_type=jnp.float32
    )
    chip = (g_mine + g_recv.astype(jnp.float32)).astype(jnp.bfloat16)
    owned = lax.psum_scatter(chip, "z", scatter_dimension=0, tiled=True)
    token_grad, owned = lax.optimization_barrier((token_grad, owned))
    owned = owned.astype(jnp.float32)
    new_weight, new_first, new_second = adamw(weight, moment_one, moment_two, owned / loss_scale)
    return (token_grad, new_weight, new_first, new_second)


def solution(mesh):
    n_expert, n_dp = mesh.devices.shape
    split_mesh = Mesh(mesh.devices.reshape(n_expert, n_dp // CORES, CORES), ("expert",) + DP)
    in_specs = (
        P(("expert",) + DP, None),
        P(DP, "expert", None, None),
        P(DP, "expert", None, None),
        P(DP, "expert"),
        P(DP, "expert"),
        P(DP, "expert"),
    )
    out_specs = (P(("expert",) + DP, None), P(DP, "expert"), P(DP, "expert"), P(DP, "expert"))
    return jax.shard_map(
        shards, mesh=split_mesh, in_specs=in_specs, out_specs=out_specs, check_vma=False
    )
```

```python
import jax
import jax.numpy as jnp
from jax import lax
from jax.sharding import Mesh
from jax.sharding import PartitionSpec as P

beta_one = 0.9
beta_two = 0.95
learn_rate = 0.003
decay = 0.1
epsilon = 1e-08
loss_scale = 64.0
bias_one = 1.0 - (0.9**50) ** 2
bias_two = 1.0 - (0.95**50) ** 2
CORES = 2
DP = ("z", "core")


def adamw(weight, moment_one, moment_two, grad):
    new_first = beta_one * moment_one + (1.0 - beta_one) * grad
    new_second = beta_two * moment_two + (1.0 - beta_two) * grad * grad
    update = new_first / bias_one / (jnp.sqrt(new_second / bias_two) + epsilon)
    new_weight = weight - learn_rate * (update + decay * weight)
    return (new_weight, new_first, new_second)


SWAP = [(0, 1), (1, 0)]


def flood_pairs(n_z, t):
    up = [(z * CORES, (z + 1) * CORES) for z in range(t - 1, n_z - 1)]
    down = [(z * CORES + 1, (z - 1) * CORES + 1) for z in range(1, n_z - t + 1)]
    return up + down


def shards(routes, expert_inputs, hidden_grad, weight, moment_one, moment_two):
    n_expert = lax.axis_size("expert")
    n_z = lax.axis_size("z")
    experts = n_expert // 2
    slot_rows = expert_inputs.shape[2]
    capacity = slot_rows // n_expert
    width = expert_inputs.shape[3]
    rows = weight.shape[0]
    tok_count = routes.shape[0]
    top_count = routes.shape[1]
    me_c = lax.axis_index("core")
    me_z = lax.axis_index("z")
    flat_routes = routes.reshape(-1)
    onehot = (flat_routes[:, None] == jnp.arange(experts, dtype=jnp.int32)[None, :]).astype(
        jnp.int32
    )
    running = jnp.cumsum(onehot, axis=0)
    slots = jnp.sum((running - 1) * onehot, axis=1).reshape(tok_count, top_count)
    counts = jnp.sum(onehot, axis=0)
    all_counts = lax.all_gather(counts[None, :], "expert", axis=0, tiled=True)
    my_expert = lax.axis_index("expert") // 2
    chosen = jnp.arange(experts, dtype=jnp.int32)[None, :] == my_expert
    my_counts = jnp.sum(jnp.where(chosen, all_counts, 0), axis=1)
    valid = (jnp.arange(capacity, dtype=jnp.int32)[None, :] < my_counts[:, None]).reshape(-1)
    inputs_flat = expert_inputs.reshape(slot_rows, width)
    grad_flat = hidden_grad.reshape(slot_rows, -1)
    masked = jnp.where(valid[:, None], grad_flat, jnp.zeros_like(grad_flat))

    wbf = weight.astype(jnp.bfloat16)
    partner = lax.ppermute(wbf, "core", SWAP)
    chip_w = jnp.where(
        me_c == 0, jnp.concatenate([wbf, partner], axis=0), jnp.concatenate([partner, wbf], axis=0)
    )
    held = []
    cur = chip_w
    for t in range(1, n_z):
        cur = lax.ppermute(cur, DP, flood_pairs(n_z, t))
        held.append(cur)
    own_held = jnp.stack(held)
    other_held = lax.ppermute(own_held, "core", SWAP)
    down_side = jnp.where(me_c == 0, own_held, other_held)
    up_side = jnp.where(me_c == 0, other_held, own_held)
    parts = [chip_w]
    for r in range(1, n_z):
        parts.append(jnp.where(me_z + r < n_z, up_side[r - 1], down_side[n_z - r - 1]))
    w_rel = jnp.concatenate(parts, axis=0)
    cols = (((1,), (1,)), ((), ()))
    partial_rows = lax.dot_general(masked, w_rel, cols, preferred_element_type=jnp.float32)
    sent = partial_rows.reshape(n_expert, capacity, width)
    received = lax.all_to_all(sent, "expert", split_axis=0, concat_axis=0, tiled=True)
    paired = jnp.sum(received.reshape(experts, 2, capacity, width), axis=1).astype(jnp.bfloat16)
    picked = paired[routes, slots]
    token_rel = jnp.sum(picked.astype(jnp.float32), axis=1).astype(jnp.bfloat16)
    token_grad = jnp.roll(token_rel.reshape(tok_count, n_z, CORES * rows), me_z, axis=1)
    token_grad = token_grad.reshape(tok_count, width)

    by_class = inputs_flat.reshape(slot_rows, n_z, CORES, rows)
    in_mine = lax.dynamic_index_in_dim(by_class, me_c, axis=2, keepdims=False)
    in_other = lax.dynamic_index_in_dim(by_class, 1 - me_c, axis=2, keepdims=False)
    dims = (((0,), (0,)), ((), ()))
    g_other = lax.dot_general(
        in_other.reshape(slot_rows, n_z * rows), masked, dims, preferred_element_type=jnp.float32
    )
    g_recv = lax.ppermute(g_other.astype(jnp.bfloat16), "core", SWAP)
    g_mine = lax.dot_general(
        in_mine.reshape(slot_rows, n_z * rows), masked, dims, preferred_element_type=jnp.float32
    )
    chip = (g_mine + g_recv.astype(jnp.float32)).astype(jnp.bfloat16)
    owned = lax.psum_scatter(chip, "z", scatter_dimension=0, tiled=True)
    token_grad, owned = lax.optimization_barrier((token_grad, owned))
    owned = owned.astype(jnp.float32)
    new_weight, new_first, new_second = adamw(weight, moment_one, moment_two, owned / loss_scale)
    return (token_grad, new_weight, new_first, new_second)


def solution(mesh):
    n_expert, n_dp = mesh.devices.shape
    split_mesh = Mesh(mesh.devices.reshape(n_expert, n_dp // CORES, CORES), ("expert",) + DP)
    in_specs = (
        P(("expert",) + DP, None),
        P(DP, "expert", None, None),
        P(DP, "expert", None, None),
        P(DP, "expert"),
        P(DP, "expert"),
        P(DP, "expert"),
    )
    out_specs = (P(("expert",) + DP, None), P(DP, "expert"), P(DP, "expert"), P(DP, "expert"))
    return jax.shard_map(
        shards, mesh=split_mesh, in_specs=in_specs, out_specs=out_specs, check_vma=False
    )
```

```python
import jax
import jax.numpy as jnp
from jax import lax
from jax.sharding import Mesh
from jax.sharding import PartitionSpec as P

beta_one = 0.9
beta_two = 0.95
learn_rate = 0.003
decay = 0.1
epsilon = 1e-08
loss_scale = 64.0
bias_one = 1.0 - (0.9**50) ** 2
bias_two = 1.0 - (0.95**50) ** 2
CORES = 2
DP = ("z", "core")


def adamw(weight, moment_one, moment_two, grad):
    new_first = beta_one * moment_one + (1.0 - beta_one) * grad
    new_second = beta_two * moment_two + (1.0 - beta_two) * grad * grad
    update = new_first / bias_one / (jnp.sqrt(new_second / bias_two) + epsilon)
    new_weight = weight - learn_rate * (update + decay * weight)
    return (new_weight, new_first, new_second)


SWAP = [(0, 1), (1, 0)]


def flood_pairs(n_z, t):
    up = [(z * CORES, (z + 1) * CORES) for z in range(t - 1, n_z - 1)]
    down = [(z * CORES + 1, (z - 1) * CORES + 1) for z in range(1, n_z - t + 1)]
    return up + down


def shards(routes, expert_inputs, hidden_grad, weight, moment_one, moment_two):
    n_expert = lax.axis_size("expert")
    n_z = lax.axis_size("z")
    experts = n_expert // 2
    slot_rows = expert_inputs.shape[2]
    capacity = slot_rows // n_expert
    width = expert_inputs.shape[3]
    rows = weight.shape[0]
    tok_count = routes.shape[0]
    top_count = routes.shape[1]
    me_c = lax.axis_index("core")
    me_z = lax.axis_index("z")
    flat_routes = routes.reshape(-1)
    onehot = (flat_routes[:, None] == jnp.arange(experts, dtype=jnp.int32)[None, :]).astype(
        jnp.int32
    )
    running = jnp.cumsum(onehot, axis=0)
    slots = jnp.sum((running - 1) * onehot, axis=1).reshape(tok_count, top_count)
    counts = jnp.sum(onehot, axis=0)
    all_counts = lax.all_gather(counts[None, :], "expert", axis=0, tiled=True)
    my_expert = lax.axis_index("expert") // 2
    chosen = jnp.arange(experts, dtype=jnp.int32)[None, :] == my_expert
    my_counts = jnp.sum(jnp.where(chosen, all_counts, 0), axis=1)
    valid = (jnp.arange(capacity, dtype=jnp.int32)[None, :] < my_counts[:, None]).reshape(-1)
    inputs_flat = expert_inputs.reshape(slot_rows, width)
    grad_flat = hidden_grad.reshape(slot_rows, -1)
    masked = jnp.where(valid[:, None], grad_flat, jnp.zeros_like(grad_flat))

    wbf = weight.astype(jnp.bfloat16)
    partner = lax.ppermute(wbf, "core", SWAP)
    chip_w = jnp.where(
        me_c == 0, jnp.concatenate([wbf, partner], axis=0), jnp.concatenate([partner, wbf], axis=0)
    )
    held = []
    cur = chip_w
    for t in range(1, n_z):
        cur = lax.ppermute(cur, DP, flood_pairs(n_z, t))
        held.append(cur)
    own_held = jnp.stack(held)
    other_held = lax.ppermute(own_held, "core", SWAP)
    down_side = jnp.where(me_c == 0, own_held, other_held)
    up_side = jnp.where(me_c == 0, other_held, own_held)
    parts = [chip_w]
    for r in range(1, n_z):
        parts.append(jnp.where(me_z + r < n_z, up_side[r - 1], down_side[n_z - r - 1]))
    w_rel = jnp.concatenate(parts, axis=0)
    cols = (((1,), (1,)), ((), ()))
    partial_rows = lax.dot_general(masked, w_rel, cols, preferred_element_type=jnp.float32)
    sent = partial_rows.reshape(n_expert, capacity, width)
    received = lax.all_to_all(sent, "expert", split_axis=0, concat_axis=0, tiled=True)
    paired = jnp.sum(received.reshape(experts, 2, capacity, width), axis=1).astype(jnp.bfloat16)
    target = (routes * capacity + slots).reshape(tok_count, top_count, 1)
    choose = jnp.sum(
        (target == jnp.arange(experts * capacity, dtype=jnp.int32)).astype(jnp.int32), axis=1
    ).astype(jnp.bfloat16)
    token_rel = jnp.dot(
        choose, paired.reshape(experts * capacity, width), preferred_element_type=jnp.float32
    ).astype(jnp.bfloat16)
    token_grad = jnp.roll(token_rel.reshape(tok_count, n_z, CORES * rows), me_z, axis=1)
    token_grad = token_grad.reshape(tok_count, width)

    by_class = inputs_flat.reshape(slot_rows, n_z, CORES, rows)
    in_mine = lax.dynamic_index_in_dim(by_class, me_c, axis=2, keepdims=False)
    in_other = lax.dynamic_index_in_dim(by_class, 1 - me_c, axis=2, keepdims=False)
    dims = (((0,), (0,)), ((), ()))
    g_other = lax.dot_general(
        in_other.reshape(slot_rows, n_z * rows), masked, dims, preferred_element_type=jnp.float32
    )
    g_recv = lax.ppermute(g_other.astype(jnp.bfloat16), "core", SWAP)
    g_mine = lax.dot_general(
        in_mine.reshape(slot_rows, n_z * rows), masked, dims, preferred_element_type=jnp.float32
    )
    chip = (g_mine + g_recv.astype(jnp.float32)).astype(jnp.bfloat16)
    owned = lax.psum_scatter(chip, "z", scatter_dimension=0, tiled=True)
    token_grad, owned = lax.optimization_barrier((token_grad, owned))
    owned = owned.astype(jnp.float32)
    new_weight, new_first, new_second = adamw(weight, moment_one, moment_two, owned / loss_scale)
    return (token_grad, new_weight, new_first, new_second)


def solution(mesh):
    n_expert, n_dp = mesh.devices.shape
    split_mesh = Mesh(mesh.devices.reshape(n_expert, n_dp // CORES, CORES), ("expert",) + DP)
    in_specs = (
        P(("expert",) + DP, None),
        P(DP, "expert", None, None),
        P(DP, "expert", None, None),
        P(DP, "expert"),
        P(DP, "expert"),
        P(DP, "expert"),
    )
    out_specs = (P(("expert",) + DP, None), P(DP, "expert"), P(DP, "expert"), P(DP, "expert"))
    return jax.shard_map(
        shards, mesh=split_mesh, in_specs=in_specs, out_specs=out_specs, check_vma=False
    )
```

```python
import jax
import jax.numpy as jnp
from jax import lax
from jax.sharding import Mesh
from jax.sharding import PartitionSpec as P

beta_one = 0.9
beta_two = 0.95
learn_rate = 0.003
decay = 0.1
epsilon = 1e-08
loss_scale = 64.0
bias_one = 1.0 - (0.9**50) ** 2
bias_two = 1.0 - (0.95**50) ** 2
CORES = 2
DP = ("z", "core")


def adamw(weight, moment_one, moment_two, grad):
    new_first = beta_one * moment_one + (1.0 - beta_one) * grad
    new_second = beta_two * moment_two + (1.0 - beta_two) * grad * grad
    update = new_first / bias_one / (jnp.sqrt(new_second / bias_two) + epsilon)
    new_weight = weight - learn_rate * (update + decay * weight)
    return (new_weight, new_first, new_second)


SWAP = [(0, 1), (1, 0)]


def flood_pairs(n_z, t):
    up = [(z * CORES, (z + 1) * CORES) for z in range(t - 1, n_z - 1)]
    down = [(z * CORES + 1, (z - 1) * CORES + 1) for z in range(1, n_z - t + 1)]
    return up + down


def shards(routes, expert_inputs, hidden_grad, weight, moment_one, moment_two):
    n_expert = lax.axis_size("expert")
    n_z = lax.axis_size("z")
    experts = n_expert // 2
    slot_rows = expert_inputs.shape[2]
    capacity = slot_rows // n_expert
    width = expert_inputs.shape[3]
    rows = weight.shape[0]
    tok_count = routes.shape[0]
    top_count = routes.shape[1]
    me_c = lax.axis_index("core")
    me_z = lax.axis_index("z")
    flat_routes = routes.reshape(-1)
    onehot = (flat_routes[:, None] == jnp.arange(experts, dtype=jnp.int32)[None, :]).astype(
        jnp.int32
    )
    running = jnp.cumsum(onehot, axis=0)
    slots = jnp.sum((running - 1) * onehot, axis=1).reshape(tok_count, top_count)
    counts = jnp.sum(onehot, axis=0)
    all_counts = lax.all_gather(counts[None, :], "expert", axis=0, tiled=True)
    my_expert = lax.axis_index("expert") // 2
    chosen = jnp.arange(experts, dtype=jnp.int32)[None, :] == my_expert
    my_counts = jnp.sum(jnp.where(chosen, all_counts, 0), axis=1)
    valid = (jnp.arange(capacity, dtype=jnp.int32)[None, :] < my_counts[:, None]).reshape(-1)
    inputs_flat = expert_inputs.reshape(slot_rows, width)
    grad_flat = hidden_grad.reshape(slot_rows, -1)
    masked = jnp.where(valid[:, None], grad_flat, jnp.zeros_like(grad_flat))

    wbf = weight.astype(jnp.bfloat16)
    partner = lax.ppermute(wbf, "core", SWAP)
    chip_w = jnp.where(
        me_c == 0, jnp.concatenate([wbf, partner], axis=0), jnp.concatenate([partner, wbf], axis=0)
    )
    held = []
    cur = chip_w
    for t in range(1, n_z):
        cur = lax.ppermute(cur, DP, flood_pairs(n_z, t))
        held.append(cur)
    other_held = lax.ppermute(tuple(held), "core", SWAP)
    parts = [chip_w]
    for r in range(1, n_z):
        up = jnp.where(me_c == 0, other_held[r - 1], held[r - 1])
        down = jnp.where(me_c == 0, held[n_z - r - 1], other_held[n_z - r - 1])
        parts.append(jnp.where(me_z + r < n_z, up, down))
    w_rel = jnp.concatenate(parts, axis=0)
    cols = (((1,), (1,)), ((), ()))
    partial_rows = lax.dot_general(masked, w_rel, cols, preferred_element_type=jnp.float32)
    sent = partial_rows.reshape(n_expert, capacity, width)
    received = lax.all_to_all(sent, "expert", split_axis=0, concat_axis=0, tiled=True)
    paired = jnp.sum(received.reshape(experts, 2, capacity, width), axis=1).astype(jnp.bfloat16)
    target = (routes * capacity + slots).reshape(tok_count, top_count, 1)
    choose = jnp.sum(
        (target == jnp.arange(experts * capacity, dtype=jnp.int32)).astype(jnp.int32), axis=1
    ).astype(jnp.bfloat16)
    token_rel = jnp.dot(
        choose, paired.reshape(experts * capacity, width), preferred_element_type=jnp.float32
    ).astype(jnp.bfloat16)
    token_grad = jnp.roll(token_rel.reshape(tok_count, n_z, CORES * rows), me_z, axis=1)
    token_grad = token_grad.reshape(tok_count, width)

    by_class = inputs_flat.reshape(slot_rows, n_z, CORES, rows)
    in_mine = lax.dynamic_index_in_dim(by_class, me_c, axis=2, keepdims=False)
    in_other = lax.dynamic_index_in_dim(by_class, 1 - me_c, axis=2, keepdims=False)
    dims = (((0,), (0,)), ((), ()))
    g_other = lax.dot_general(
        in_other.reshape(slot_rows, n_z * rows), masked, dims, preferred_element_type=jnp.float32
    )
    g_recv = lax.ppermute(g_other.astype(jnp.bfloat16), "core", SWAP)
    g_mine = lax.dot_general(
        in_mine.reshape(slot_rows, n_z * rows), masked, dims, preferred_element_type=jnp.float32
    )
    chip = (g_mine + g_recv.astype(jnp.float32)).astype(jnp.bfloat16)
    owned = lax.psum_scatter(chip, "z", scatter_dimension=0, tiled=True)
    token_grad, owned = lax.optimization_barrier((token_grad, owned))
    owned = owned.astype(jnp.float32)
    new_weight, new_first, new_second = adamw(weight, moment_one, moment_two, owned / loss_scale)
    return (token_grad, new_weight, new_first, new_second)


def solution(mesh):
    n_expert, n_dp = mesh.devices.shape
    split_mesh = Mesh(mesh.devices.reshape(n_expert, n_dp // CORES, CORES), ("expert",) + DP)
    in_specs = (
        P(("expert",) + DP, None),
        P(DP, "expert", None, None),
        P(DP, "expert", None, None),
        P(DP, "expert"),
        P(DP, "expert"),
        P(DP, "expert"),
    )
    out_specs = (P(("expert",) + DP, None), P(DP, "expert"), P(DP, "expert"), P(DP, "expert"))
    return jax.shard_map(
        shards, mesh=split_mesh, in_specs=in_specs, out_specs=out_specs, check_vma=False
    )
```

```python
import jax
import jax.numpy as jnp
from jax import lax
from jax.sharding import Mesh
from jax.sharding import PartitionSpec as P

beta_one = 0.9
beta_two = 0.95
learn_rate = 0.003
decay = 0.1
epsilon = 1e-08
loss_scale = 64.0
bias_one = 1.0 - (0.9**50) ** 2
bias_two = 1.0 - (0.95**50) ** 2
CORES = 2
DP = ("z", "core")


def adamw(weight, moment_one, moment_two, grad):
    new_first = beta_one * moment_one + (1.0 - beta_one) * grad
    new_second = beta_two * moment_two + (1.0 - beta_two) * grad * grad
    update = new_first / bias_one / (jnp.sqrt(new_second / bias_two) + epsilon)
    new_weight = weight - learn_rate * (update + decay * weight)
    return (new_weight, new_first, new_second)


SWAP = [(0, 1), (1, 0)]


def flood_pairs(n_z, t):
    up = [(z * CORES, (z + 1) * CORES) for z in range(t - 1, n_z - 1)]
    down = [(z * CORES + 1, (z - 1) * CORES + 1) for z in range(1, n_z - t + 1)]
    return up + down


def shards(routes, expert_inputs, hidden_grad, weight, moment_one, moment_two):
    n_expert = lax.axis_size("expert")
    n_z = lax.axis_size("z")
    experts = n_expert // 2
    slot_rows = expert_inputs.shape[2]
    capacity = slot_rows // n_expert
    width = expert_inputs.shape[3]
    rows = weight.shape[0]
    tok_count = routes.shape[0]
    top_count = routes.shape[1]
    me_c = lax.axis_index("core")
    me_z = lax.axis_index("z")
    flat_routes = routes.reshape(-1)
    onehot = (flat_routes[:, None] == jnp.arange(experts, dtype=jnp.int32)[None, :]).astype(
        jnp.int32
    )
    running = jnp.cumsum(onehot, axis=0)
    slots = jnp.sum((running - 1) * onehot, axis=1).reshape(tok_count, top_count)
    counts = jnp.sum(onehot, axis=0)
    all_counts = lax.all_gather(counts[None, :], "expert", axis=0, tiled=True)
    my_expert = lax.axis_index("expert") // 2
    chosen = jnp.arange(experts, dtype=jnp.int32)[None, :] == my_expert
    my_counts = jnp.sum(jnp.where(chosen, all_counts, 0), axis=1)
    valid = (jnp.arange(capacity, dtype=jnp.int32)[None, :] < my_counts[:, None]).reshape(-1)
    inputs_flat = expert_inputs.reshape(slot_rows, width)
    grad_flat = hidden_grad.reshape(slot_rows, -1)
    masked = jnp.where(valid[:, None], grad_flat, jnp.zeros_like(grad_flat))

    wbf = weight.astype(jnp.bfloat16)
    partner = lax.ppermute(wbf, "core", SWAP)
    chip_w = jnp.where(
        me_c == 0, jnp.concatenate([wbf, partner], axis=0), jnp.concatenate([partner, wbf], axis=0)
    )
    held = []
    cur = chip_w
    for t in range(1, n_z):
        cur = lax.ppermute(cur, DP, flood_pairs(n_z, t))
        held.append(cur)
    held = lax.optimization_barrier(tuple(held))
    other_held = lax.ppermute(held, "core", SWAP)
    parts = [chip_w]
    for r in range(1, n_z):
        up = jnp.where(me_c == 0, other_held[r - 1], held[r - 1])
        down = jnp.where(me_c == 0, held[n_z - r - 1], other_held[n_z - r - 1])
        parts.append(jnp.where(me_z + r < n_z, up, down))
    w_rel = jnp.concatenate(parts, axis=0)
    cols = (((1,), (1,)), ((), ()))
    partial_rows = lax.dot_general(masked, w_rel, cols, preferred_element_type=jnp.float32)
    sent = partial_rows.reshape(n_expert, capacity, width)
    received = lax.all_to_all(sent, "expert", split_axis=0, concat_axis=0, tiled=True)
    paired = jnp.sum(received.reshape(experts, 2, capacity, width), axis=1).astype(jnp.bfloat16)
    target = (routes * capacity + slots).reshape(tok_count, top_count, 1)
    choose = jnp.sum(
        (target == jnp.arange(experts * capacity, dtype=jnp.int32)).astype(jnp.int32), axis=1
    ).astype(jnp.bfloat16)
    token_rel = jnp.dot(
        choose, paired.reshape(experts * capacity, width), preferred_element_type=jnp.float32
    ).astype(jnp.bfloat16)
    token_grad = jnp.roll(token_rel.reshape(tok_count, n_z, CORES * rows), me_z, axis=1)
    token_grad = token_grad.reshape(tok_count, width)

    by_class = inputs_flat.reshape(slot_rows, n_z, CORES, rows)
    in_mine = lax.dynamic_index_in_dim(by_class, me_c, axis=2, keepdims=False)
    in_other = lax.dynamic_index_in_dim(by_class, 1 - me_c, axis=2, keepdims=False)
    dims = (((0,), (0,)), ((), ()))
    g_other = lax.dot_general(
        in_other.reshape(slot_rows, n_z * rows), masked, dims, preferred_element_type=jnp.float32
    )
    g_recv = lax.ppermute(g_other.astype(jnp.bfloat16), "core", SWAP)
    g_mine = lax.dot_general(
        in_mine.reshape(slot_rows, n_z * rows), masked, dims, preferred_element_type=jnp.float32
    )
    chip = (g_mine + g_recv.astype(jnp.float32)).astype(jnp.bfloat16)
    owned = lax.psum_scatter(chip, "z", scatter_dimension=0, tiled=True)
    token_grad, owned = lax.optimization_barrier((token_grad, owned))
    owned = owned.astype(jnp.float32)
    new_weight, new_first, new_second = adamw(weight, moment_one, moment_two, owned / loss_scale)
    return (token_grad, new_weight, new_first, new_second)


def solution(mesh):
    n_expert, n_dp = mesh.devices.shape
    split_mesh = Mesh(mesh.devices.reshape(n_expert, n_dp // CORES, CORES), ("expert",) + DP)
    in_specs = (
        P(("expert",) + DP, None),
        P(DP, "expert", None, None),
        P(DP, "expert", None, None),
        P(DP, "expert"),
        P(DP, "expert"),
        P(DP, "expert"),
    )
    out_specs = (P(("expert",) + DP, None), P(DP, "expert"), P(DP, "expert"), P(DP, "expert"))
    return jax.shard_map(
        shards, mesh=split_mesh, in_specs=in_specs, out_specs=out_specs, check_vma=False
    )
```

```python
import jax
import jax.numpy as jnp
from jax import lax
from jax.sharding import Mesh
from jax.sharding import PartitionSpec as P

beta_one = 0.9
beta_two = 0.95
learn_rate = 0.003
decay = 0.1
epsilon = 1e-08
loss_scale = 64.0
bias_one = 1.0 - (0.9**50) ** 2
bias_two = 1.0 - (0.95**50) ** 2
CORES = 2
DP = ("z", "core")


def adamw(weight, moment_one, moment_two, grad):
    new_first = beta_one * moment_one + (1.0 - beta_one) * grad
    new_second = beta_two * moment_two + (1.0 - beta_two) * grad * grad
    update = new_first / bias_one / (jnp.sqrt(new_second / bias_two) + epsilon)
    new_weight = weight - learn_rate * (update + decay * weight)
    return (new_weight, new_first, new_second)


SWAP = [(0, 1), (1, 0)]


def flood_pairs(n_z, t):
    up = [(z * CORES, (z + 1) * CORES) for z in range(t - 1, n_z - 1)]
    down = [(z * CORES + 1, (z - 1) * CORES + 1) for z in range(1, n_z - t + 1)]
    return up + down


def shards(routes, expert_inputs, hidden_grad, weight, moment_one, moment_two):
    n_expert = lax.axis_size("expert")
    n_z = lax.axis_size("z")
    experts = n_expert // 2
    slot_rows = expert_inputs.shape[2]
    capacity = slot_rows // n_expert
    width = expert_inputs.shape[3]
    rows = weight.shape[0]
    tok_count = routes.shape[0]
    top_count = routes.shape[1]
    me_c = lax.axis_index("core")
    me_z = lax.axis_index("z")
    flat_routes = routes.reshape(-1)
    onehot = (flat_routes[:, None] == jnp.arange(experts, dtype=jnp.int32)[None, :]).astype(
        jnp.int32
    )
    running = jnp.cumsum(onehot, axis=0)
    slots = jnp.sum((running - 1) * onehot, axis=1).reshape(tok_count, top_count)
    counts = jnp.sum(onehot, axis=0)
    all_counts = lax.all_gather(counts[None, :], "expert", axis=0, tiled=True)
    my_expert = lax.axis_index("expert") // 2
    chosen = jnp.arange(experts, dtype=jnp.int32)[None, :] == my_expert
    my_counts = jnp.sum(jnp.where(chosen, all_counts, 0), axis=1)
    valid = (jnp.arange(capacity, dtype=jnp.int32)[None, :] < my_counts[:, None]).reshape(-1)
    inputs_flat = expert_inputs.reshape(slot_rows, width)
    grad_flat = hidden_grad.reshape(slot_rows, -1)
    masked = jnp.where(valid[:, None], grad_flat, jnp.zeros_like(grad_flat))

    wbf = weight.astype(jnp.bfloat16)
    partner = lax.ppermute(wbf, "core", SWAP)
    chip_w = jnp.where(
        me_c == 0, jnp.concatenate([wbf, partner], axis=0), jnp.concatenate([partner, wbf], axis=0)
    )
    held = []
    cur = chip_w
    for t in range(1, n_z):
        cur = lax.ppermute(cur, DP, flood_pairs(n_z, t))
        held.append(cur)
    by_class = inputs_flat.reshape(slot_rows, n_z, CORES, rows)
    in_mine = lax.dynamic_index_in_dim(by_class, me_c, axis=2, keepdims=False)
    in_other = lax.dynamic_index_in_dim(by_class, 1 - me_c, axis=2, keepdims=False)
    dims = (((0,), (0,)), ((), ()))
    g_other = lax.dot_general(
        in_other.reshape(slot_rows, n_z * rows), masked, dims, preferred_element_type=jnp.float32
    )
    g_recv = lax.ppermute(g_other.astype(jnp.bfloat16), "core", SWAP)
    g_mine = lax.dot_general(
        in_mine.reshape(slot_rows, n_z * rows), masked, dims, preferred_element_type=jnp.float32
    )
    chip = (g_mine + g_recv.astype(jnp.float32)).astype(jnp.bfloat16)
    held, chip = lax.optimization_barrier((tuple(held), chip))
    owned = lax.psum_scatter(chip, "z", scatter_dimension=0, tiled=True)
    other_held = lax.ppermute(held, "core", SWAP)
    parts = [chip_w]
    for r in range(1, n_z):
        up = jnp.where(me_c == 0, other_held[r - 1], held[r - 1])
        down = jnp.where(me_c == 0, held[n_z - r - 1], other_held[n_z - r - 1])
        parts.append(jnp.where(me_z + r < n_z, up, down))
    w_rel = jnp.concatenate(parts, axis=0)
    cols = (((1,), (1,)), ((), ()))
    partial_rows = lax.dot_general(masked, w_rel, cols, preferred_element_type=jnp.float32)
    sent = partial_rows.reshape(n_expert, capacity, width)
    received = lax.all_to_all(sent, "expert", split_axis=0, concat_axis=0, tiled=True)
    paired = jnp.sum(received.reshape(experts, 2, capacity, width), axis=1).astype(jnp.bfloat16)
    target = (routes * capacity + slots).reshape(tok_count, top_count, 1)
    choose = jnp.sum(
        (target == jnp.arange(experts * capacity, dtype=jnp.int32)).astype(jnp.int32), axis=1
    ).astype(jnp.bfloat16)
    token_rel = jnp.dot(
        choose, paired.reshape(experts * capacity, width), preferred_element_type=jnp.float32
    ).astype(jnp.bfloat16)
    token_grad = jnp.roll(token_rel.reshape(tok_count, n_z, CORES * rows), me_z, axis=1)
    token_grad = token_grad.reshape(tok_count, width)

    token_grad, owned = lax.optimization_barrier((token_grad, owned))
    owned = owned.astype(jnp.float32)
    new_weight, new_first, new_second = adamw(weight, moment_one, moment_two, owned / loss_scale)
    return (token_grad, new_weight, new_first, new_second)


def solution(mesh):
    n_expert, n_dp = mesh.devices.shape
    split_mesh = Mesh(mesh.devices.reshape(n_expert, n_dp // CORES, CORES), ("expert",) + DP)
    in_specs = (
        P(("expert",) + DP, None),
        P(DP, "expert", None, None),
        P(DP, "expert", None, None),
        P(DP, "expert"),
        P(DP, "expert"),
        P(DP, "expert"),
    )
    out_specs = (P(("expert",) + DP, None), P(DP, "expert"), P(DP, "expert"), P(DP, "expert"))
    return jax.shard_map(
        shards, mesh=split_mesh, in_specs=in_specs, out_specs=out_specs, check_vma=False
    )
```

```python
import jax
import jax.numpy as jnp
from jax import lax
from jax.sharding import Mesh
from jax.sharding import PartitionSpec as P

beta_one = 0.9
beta_two = 0.95
learn_rate = 0.003
decay = 0.1
epsilon = 1e-08
loss_scale = 64.0
bias_one = 1.0 - (0.9**50) ** 2
bias_two = 1.0 - (0.95**50) ** 2
CORES = 2
DP = ("z", "core")


def adamw(weight, moment_one, moment_two, grad):
    new_first = beta_one * moment_one + (1.0 - beta_one) * grad
    new_second = beta_two * moment_two + (1.0 - beta_two) * grad * grad
    update = new_first / bias_one / (jnp.sqrt(new_second / bias_two) + epsilon)
    new_weight = weight - learn_rate * (update + decay * weight)
    return (new_weight, new_first, new_second)


SWAP = [(0, 1), (1, 0)]


def flood_pairs(n_z, t):
    up = [(z * CORES, (z + 1) * CORES) for z in range(t - 1, n_z - 1)]
    down = [(z * CORES + 1, (z - 1) * CORES + 1) for z in range(1, n_z - t + 1)]
    return up + down


def shards(routes, expert_inputs, hidden_grad, weight, moment_one, moment_two):
    n_expert = lax.axis_size("expert")
    n_z = lax.axis_size("z")
    experts = n_expert // 2
    slot_rows = expert_inputs.shape[2]
    capacity = slot_rows // n_expert
    width = expert_inputs.shape[3]
    rows = weight.shape[0]
    tok_count = routes.shape[0]
    top_count = routes.shape[1]
    me_c = lax.axis_index("core")
    me_z = lax.axis_index("z")
    flat_routes = routes.reshape(-1)
    onehot = (flat_routes[:, None] == jnp.arange(experts, dtype=jnp.int32)[None, :]).astype(
        jnp.int32
    )
    running = jnp.cumsum(onehot, axis=0)
    slots = jnp.sum((running - 1) * onehot, axis=1).reshape(tok_count, top_count)
    counts = jnp.sum(onehot, axis=0)
    all_counts = lax.all_gather(counts[None, :], "expert", axis=0, tiled=True)
    my_expert = lax.axis_index("expert") // 2
    chosen = jnp.arange(experts, dtype=jnp.int32)[None, :] == my_expert
    my_counts = jnp.sum(jnp.where(chosen, all_counts, 0), axis=1)
    valid = (jnp.arange(capacity, dtype=jnp.int32)[None, :] < my_counts[:, None]).reshape(-1)
    inputs_flat = expert_inputs.reshape(slot_rows, width)
    grad_flat = hidden_grad.reshape(slot_rows, -1)
    masked = jnp.where(valid[:, None], grad_flat, jnp.zeros_like(grad_flat))

    wbf = weight.astype(jnp.bfloat16)
    partner = lax.ppermute(wbf, "core", SWAP)
    chip_w = jnp.where(
        me_c == 0, jnp.concatenate([wbf, partner], axis=0), jnp.concatenate([partner, wbf], axis=0)
    )
    held = []
    cur = chip_w
    for t in range(1, n_z):
        cur = lax.ppermute(cur, DP, flood_pairs(n_z, t))
        held.append(cur)
    by_class = inputs_flat.reshape(slot_rows, n_z, CORES, rows)
    in_mine = lax.dynamic_index_in_dim(by_class, me_c, axis=2, keepdims=False)
    in_other = lax.dynamic_index_in_dim(by_class, 1 - me_c, axis=2, keepdims=False)
    dims = (((0,), (0,)), ((), ()))
    g_other = lax.dot_general(
        in_other.reshape(slot_rows, n_z * rows), masked, dims, preferred_element_type=jnp.float32
    )
    g_recv = lax.ppermute(g_other.astype(jnp.bfloat16), "core", SWAP)
    g_mine = lax.dot_general(
        in_mine.reshape(slot_rows, n_z * rows), masked, dims, preferred_element_type=jnp.float32
    )
    chip = (g_mine + g_recv.astype(jnp.float32)).astype(jnp.bfloat16)
    held, chip = lax.optimization_barrier((tuple(held), chip))
    owned = lax.psum_scatter(chip, "z", scatter_dimension=0, tiled=True)
    other_held = lax.ppermute(held, "core", SWAP)
    cols = (((1,), (1,)), ((), ()))
    own_rows = lax.dot_general(masked, chip_w, cols, preferred_element_type=jnp.float32)
    recv_own = lax.all_to_all(
        own_rows.reshape(n_expert, capacity, CORES * rows), "expert", 0, 0, tiled=True
    )
    parts = []
    for r in range(1, n_z):
        up = jnp.where(me_c == 0, other_held[r - 1], held[r - 1])
        down = jnp.where(me_c == 0, held[n_z - r - 1], other_held[n_z - r - 1])
        parts.append(jnp.where(me_z + r < n_z, up, down))
    w_rest = jnp.concatenate(parts, axis=0)
    rest_rows = lax.dot_general(masked, w_rest, cols, preferred_element_type=jnp.float32)
    recv_rest = lax.all_to_all(
        rest_rows.reshape(n_expert, capacity, width - CORES * rows), "expert", 0, 0, tiled=True
    )
    received = jnp.concatenate([recv_own, recv_rest], axis=2)
    paired = jnp.sum(received.reshape(experts, 2, capacity, width), axis=1).astype(jnp.bfloat16)
    target = (routes * capacity + slots).reshape(tok_count, top_count, 1)
    choose = jnp.sum(
        (target == jnp.arange(experts * capacity, dtype=jnp.int32)).astype(jnp.int32), axis=1
    ).astype(jnp.bfloat16)
    token_rel = jnp.dot(
        choose, paired.reshape(experts * capacity, width), preferred_element_type=jnp.float32
    ).astype(jnp.bfloat16)
    token_grad = jnp.roll(token_rel.reshape(tok_count, n_z, CORES * rows), me_z, axis=1)
    token_grad = token_grad.reshape(tok_count, width)

    token_grad, owned = lax.optimization_barrier((token_grad, owned))
    owned = owned.astype(jnp.float32)
    new_weight, new_first, new_second = adamw(weight, moment_one, moment_two, owned / loss_scale)
    return (token_grad, new_weight, new_first, new_second)


def solution(mesh):
    n_expert, n_dp = mesh.devices.shape
    split_mesh = Mesh(mesh.devices.reshape(n_expert, n_dp // CORES, CORES), ("expert",) + DP)
    in_specs = (
        P(("expert",) + DP, None),
        P(DP, "expert", None, None),
        P(DP, "expert", None, None),
        P(DP, "expert"),
        P(DP, "expert"),
        P(DP, "expert"),
    )
    out_specs = (P(("expert",) + DP, None), P(DP, "expert"), P(DP, "expert"), P(DP, "expert"))
    return jax.shard_map(
        shards, mesh=split_mesh, in_specs=in_specs, out_specs=out_specs, check_vma=False
    )
```

```python
import jax
import jax.numpy as jnp
from jax import lax
from jax.sharding import Mesh
from jax.sharding import PartitionSpec as P

beta_one = 0.9
beta_two = 0.95
learn_rate = 0.003
decay = 0.1
epsilon = 1e-08
loss_scale = 64.0
bias_one = 1.0 - (0.9**50) ** 2
bias_two = 1.0 - (0.95**50) ** 2
CORES = 2
DP = ("z", "core")


def adamw(weight, moment_one, moment_two, grad):
    new_first = beta_one * moment_one + (1.0 - beta_one) * grad
    new_second = beta_two * moment_two + (1.0 - beta_two) * grad * grad
    update = new_first / bias_one / (jnp.sqrt(new_second / bias_two) + epsilon)
    new_weight = weight - learn_rate * (update + decay * weight)
    return (new_weight, new_first, new_second)


SWAP = [(0, 1), (1, 0)]


def flood_pairs(n_z, t):
    up = [(z * CORES, (z + 1) * CORES) for z in range(t - 1, n_z - 1)]
    down = [(z * CORES + 1, (z - 1) * CORES + 1) for z in range(1, n_z - t + 1)]
    return up + down


def reduce_scatter_rows(full, axis, n, me, rows):
    def own_block(q):
        q = jnp.clip(q, 0, n - 1)
        return lax.dynamic_slice_in_dim(full, q * rows, rows, axis=0)

    recv_r = None
    recv_l = None
    for t in range(1, n):
        pay_r = own_block(me + n - t)
        pay_l = own_block(me - n + t)
        if recv_r is not None:
            pay_r = pay_r + recv_r.astype(jnp.float32)
            pay_l = pay_l + recv_l.astype(jnp.float32)
        recv_r = lax.ppermute(pay_r.astype(jnp.bfloat16), axis, [(p, p + 1) for p in range(0, t)])
        recv_l = lax.ppermute(pay_l.astype(jnp.bfloat16), axis, [(p, p - 1) for p in range(n - t, n)])
    total = own_block(me)
    if recv_r is not None:
        total = total + recv_r.astype(jnp.float32) + recv_l.astype(jnp.float32)
    return total


def shards(routes, expert_inputs, hidden_grad, weight, moment_one, moment_two):
    n_expert = lax.axis_size("expert")
    n_z = lax.axis_size("z")
    experts = n_expert // 2
    slot_rows = expert_inputs.shape[2]
    capacity = slot_rows // n_expert
    width = expert_inputs.shape[3]
    rows = weight.shape[0]
    tok_count = routes.shape[0]
    top_count = routes.shape[1]
    me_c = lax.axis_index("core")
    me_z = lax.axis_index("z")
    flat_routes = routes.reshape(-1)
    onehot = (flat_routes[:, None] == jnp.arange(experts, dtype=jnp.int32)[None, :]).astype(
        jnp.int32
    )
    running = jnp.cumsum(onehot, axis=0)
    slots = jnp.sum((running - 1) * onehot, axis=1).reshape(tok_count, top_count)
    counts = jnp.sum(onehot, axis=0)
    all_counts = lax.all_gather(counts[None, :], "expert", axis=0, tiled=True)
    my_expert = lax.axis_index("expert") // 2
    chosen = jnp.arange(experts, dtype=jnp.int32)[None, :] == my_expert
    my_counts = jnp.sum(jnp.where(chosen, all_counts, 0), axis=1)
    valid = (jnp.arange(capacity, dtype=jnp.int32)[None, :] < my_counts[:, None]).reshape(-1)
    inputs_flat = expert_inputs.reshape(slot_rows, width)
    grad_flat = hidden_grad.reshape(slot_rows, -1)
    masked = jnp.where(valid[:, None], grad_flat, jnp.zeros_like(grad_flat))

    wbf = weight.astype(jnp.bfloat16)
    partner = lax.ppermute(wbf, "core", SWAP)
    chip_w = jnp.where(
        me_c == 0, jnp.concatenate([wbf, partner], axis=0), jnp.concatenate([partner, wbf], axis=0)
    )
    held = []
    cur = chip_w
    for t in range(1, n_z):
        cur = lax.ppermute(cur, DP, flood_pairs(n_z, t))
        held.append(cur)
    by_class = inputs_flat.reshape(slot_rows, n_z, CORES, rows)
    in_mine = lax.dynamic_index_in_dim(by_class, me_c, axis=2, keepdims=False)
    in_other = lax.dynamic_index_in_dim(by_class, 1 - me_c, axis=2, keepdims=False)
    dims = (((0,), (0,)), ((), ()))
    g_other = lax.dot_general(
        in_other.reshape(slot_rows, n_z * rows), masked, dims, preferred_element_type=jnp.float32
    )
    g_recv = lax.ppermute(g_other.astype(jnp.bfloat16), "core", SWAP)
    g_mine = lax.dot_general(
        in_mine.reshape(slot_rows, n_z * rows), masked, dims, preferred_element_type=jnp.float32
    )
    chip = g_mine + g_recv.astype(jnp.float32)
    held, chip = lax.optimization_barrier((tuple(held), chip))
    owned = reduce_scatter_rows(chip, "z", n_z, me_z, rows)
    other_held = lax.ppermute(held, "core", SWAP)
    cols = (((1,), (1,)), ((), ()))
    own_rows = lax.dot_general(masked, chip_w, cols, preferred_element_type=jnp.float32)
    recv_own = lax.all_to_all(
        own_rows.reshape(n_expert, capacity, CORES * rows), "expert", 0, 0, tiled=True
    )
    parts = []
    for r in range(1, n_z):
        up = jnp.where(me_c == 0, other_held[r - 1], held[r - 1])
        down = jnp.where(me_c == 0, held[n_z - r - 1], other_held[n_z - r - 1])
        parts.append(jnp.where(me_z + r < n_z, up, down))
    w_rest = jnp.concatenate(parts, axis=0)
    rest_rows = lax.dot_general(masked, w_rest, cols, preferred_element_type=jnp.float32)
    recv_rest = lax.all_to_all(
        rest_rows.reshape(n_expert, capacity, width - CORES * rows), "expert", 0, 0, tiled=True
    )
    received = jnp.concatenate([recv_own, recv_rest], axis=2)
    paired = jnp.sum(received.reshape(experts, 2, capacity, width), axis=1).astype(jnp.bfloat16)
    target = (routes * capacity + slots).reshape(tok_count, top_count, 1)
    choose = jnp.sum(
        (target == jnp.arange(experts * capacity, dtype=jnp.int32)).astype(jnp.int32), axis=1
    ).astype(jnp.bfloat16)
    token_rel = jnp.dot(
        choose, paired.reshape(experts * capacity, width), preferred_element_type=jnp.float32
    ).astype(jnp.bfloat16)
    token_grad = jnp.roll(token_rel.reshape(tok_count, n_z, CORES * rows), me_z, axis=1)
    token_grad = token_grad.reshape(tok_count, width)

    token_grad, owned = lax.optimization_barrier((token_grad, owned))
    owned = owned.astype(jnp.float32)
    new_weight, new_first, new_second = adamw(weight, moment_one, moment_two, owned / loss_scale)
    return (token_grad, new_weight, new_first, new_second)


def solution(mesh):
    n_expert, n_dp = mesh.devices.shape
    split_mesh = Mesh(mesh.devices.reshape(n_expert, n_dp // CORES, CORES), ("expert",) + DP)
    in_specs = (
        P(("expert",) + DP, None),
        P(DP, "expert", None, None),
        P(DP, "expert", None, None),
        P(DP, "expert"),
        P(DP, "expert"),
        P(DP, "expert"),
    )
    out_specs = (P(("expert",) + DP, None), P(DP, "expert"), P(DP, "expert"), P(DP, "expert"))
    return jax.shard_map(
        shards, mesh=split_mesh, in_specs=in_specs, out_specs=out_specs, check_vma=False
    )
```

```python
import jax
import jax.numpy as jnp
from jax import lax
from jax.sharding import Mesh
from jax.sharding import PartitionSpec as P

beta_one = 0.9
beta_two = 0.95
learn_rate = 0.003
decay = 0.1
epsilon = 1e-08
loss_scale = 64.0
bias_one = 1.0 - (0.9**50) ** 2
bias_two = 1.0 - (0.95**50) ** 2
CORES = 2
DP = ("z", "core")


def adamw(weight, moment_one, moment_two, grad):
    new_first = beta_one * moment_one + (1.0 - beta_one) * grad
    new_second = beta_two * moment_two + (1.0 - beta_two) * grad * grad
    update = new_first / bias_one / (jnp.sqrt(new_second / bias_two) + epsilon)
    new_weight = weight - learn_rate * (update + decay * weight)
    return (new_weight, new_first, new_second)


SWAP = [(0, 1), (1, 0)]


def flood_pairs(n_z, t):
    up = [(z * CORES, (z + 1) * CORES) for z in range(t - 1, n_z - 1)]
    down = [(z * CORES + 1, (z - 1) * CORES + 1) for z in range(1, n_z - t + 1)]
    return up + down


def shards(routes, expert_inputs, hidden_grad, weight, moment_one, moment_two):
    n_expert = lax.axis_size("expert")
    n_z = lax.axis_size("z")
    experts = n_expert // 2
    slot_rows = expert_inputs.shape[2]
    capacity = slot_rows // n_expert
    width = expert_inputs.shape[3]
    rows = weight.shape[0]
    tok_count = routes.shape[0]
    top_count = routes.shape[1]
    me_c = lax.axis_index("core")
    me_z = lax.axis_index("z")
    flat_routes = routes.reshape(-1)
    onehot = (flat_routes[:, None] == jnp.arange(experts, dtype=jnp.int32)[None, :]).astype(
        jnp.int32
    )
    running = jnp.cumsum(onehot, axis=0)
    slots = jnp.sum((running - 1) * onehot, axis=1).reshape(tok_count, top_count)
    counts = jnp.sum(onehot, axis=0)
    all_counts = lax.all_gather(counts[None, :], "expert", axis=0, tiled=True)
    my_expert = lax.axis_index("expert") // 2
    chosen = jnp.arange(experts, dtype=jnp.int32)[None, :] == my_expert
    my_counts = jnp.sum(jnp.where(chosen, all_counts, 0), axis=1)
    valid = (jnp.arange(capacity, dtype=jnp.int32)[None, :] < my_counts[:, None]).reshape(-1)
    inputs_flat = expert_inputs.reshape(slot_rows, width)
    grad_flat = hidden_grad.reshape(slot_rows, -1)
    masked = jnp.where(valid[:, None], grad_flat, jnp.zeros_like(grad_flat))

    wbf = weight.astype(jnp.bfloat16)
    partner = lax.ppermute(wbf, "core", SWAP)
    chip_w = jnp.where(
        me_c == 0, jnp.concatenate([wbf, partner], axis=0), jnp.concatenate([partner, wbf], axis=0)
    )
    held = []
    cur = chip_w
    for t in range(1, n_z):
        cur = lax.ppermute(cur, DP, flood_pairs(n_z, t))
        held.append(cur)
    dims = (((0,), (0,)), ((), ()))
    chip = lax.dot_general(
        inputs_flat, masked, dims, preferred_element_type=jnp.float32
    ).astype(jnp.bfloat16)
    held, chip = lax.optimization_barrier((tuple(held), chip))
    owned = lax.psum_scatter(chip, DP, scatter_dimension=0, tiled=True)
    other_held = lax.ppermute(held, "core", SWAP)
    cols = (((1,), (1,)), ((), ()))
    own_rows = lax.dot_general(masked, chip_w, cols, preferred_element_type=jnp.float32)
    recv_own = lax.all_to_all(
        own_rows.reshape(n_expert, capacity, CORES * rows), "expert", 0, 0, tiled=True
    )
    parts = []
    for r in range(1, n_z):
        up = jnp.where(me_c == 0, other_held[r - 1], held[r - 1])
        down = jnp.where(me_c == 0, held[n_z - r - 1], other_held[n_z - r - 1])
        parts.append(jnp.where(me_z + r < n_z, up, down))
    w_rest = jnp.concatenate(parts, axis=0)
    rest_rows = lax.dot_general(masked, w_rest, cols, preferred_element_type=jnp.float32)
    recv_rest = lax.all_to_all(
        rest_rows.reshape(n_expert, capacity, width - CORES * rows), "expert", 0, 0, tiled=True
    )
    received = jnp.concatenate([recv_own, recv_rest], axis=2)
    paired = jnp.sum(received.reshape(experts, 2, capacity, width), axis=1).astype(jnp.bfloat16)
    target = (routes * capacity + slots).reshape(tok_count, top_count, 1)
    choose = jnp.sum(
        (target == jnp.arange(experts * capacity, dtype=jnp.int32)).astype(jnp.int32), axis=1
    ).astype(jnp.bfloat16)
    token_rel = jnp.dot(
        choose, paired.reshape(experts * capacity, width), preferred_element_type=jnp.float32
    ).astype(jnp.bfloat16)
    token_grad = jnp.roll(token_rel.reshape(tok_count, n_z, CORES * rows), me_z, axis=1)
    token_grad = token_grad.reshape(tok_count, width)

    token_grad, owned = lax.optimization_barrier((token_grad, owned))
    owned = owned.astype(jnp.float32)
    new_weight, new_first, new_second = adamw(weight, moment_one, moment_two, owned / loss_scale)
    return (token_grad, new_weight, new_first, new_second)


def solution(mesh):
    n_expert, n_dp = mesh.devices.shape
    split_mesh = Mesh(mesh.devices.reshape(n_expert, n_dp // CORES, CORES), ("expert",) + DP)
    in_specs = (
        P(("expert",) + DP, None),
        P(DP, "expert", None, None),
        P(DP, "expert", None, None),
        P(DP, "expert"),
        P(DP, "expert"),
        P(DP, "expert"),
    )
    out_specs = (P(("expert",) + DP, None), P(DP, "expert"), P(DP, "expert"), P(DP, "expert"))
    return jax.shard_map(
        shards, mesh=split_mesh, in_specs=in_specs, out_specs=out_specs, check_vma=False
    )
```

```python
import jax
import jax.numpy as jnp
from jax import lax
from jax.sharding import Mesh
from jax.sharding import PartitionSpec as P

beta_one = 0.9
beta_two = 0.95
learn_rate = 0.003
decay = 0.1
epsilon = 1e-08
loss_scale = 64.0
bias_one = 1.0 - (0.9**50) ** 2
bias_two = 1.0 - (0.95**50) ** 2
CORES = 2
DP = ("z", "core")


def adamw(weight, moment_one, moment_two, grad):
    new_first = beta_one * moment_one + (1.0 - beta_one) * grad
    new_second = beta_two * moment_two + (1.0 - beta_two) * grad * grad
    update = new_first / bias_one / (jnp.sqrt(new_second / bias_two) + epsilon)
    new_weight = weight - learn_rate * (update + decay * weight)
    return (new_weight, new_first, new_second)


SWAP = [(0, 1), (1, 0)]


def flood_pairs(n_z, t):
    up = [(z * CORES, (z + 1) * CORES) for z in range(t - 1, n_z - 1)]
    down = [(z * CORES + 1, (z - 1) * CORES + 1) for z in range(1, n_z - t + 1)]
    return up + down


def shards(routes, expert_inputs, hidden_grad, weight, moment_one, moment_two):
    n_expert = lax.axis_size("expert")
    n_z = lax.axis_size("z")
    experts = n_expert // 2
    slot_rows = expert_inputs.shape[2]
    capacity = slot_rows // n_expert
    width = expert_inputs.shape[3]
    rows = weight.shape[0]
    tok_count = routes.shape[0]
    top_count = routes.shape[1]
    me_c = lax.axis_index("core")
    me_z = lax.axis_index("z")
    flat_routes = routes.reshape(-1)
    onehot = (flat_routes[:, None] == jnp.arange(experts, dtype=jnp.int32)[None, :]).astype(
        jnp.int32
    )
    running = jnp.cumsum(onehot, axis=0)
    slots = jnp.sum((running - 1) * onehot, axis=1).reshape(tok_count, top_count)
    counts = jnp.sum(onehot, axis=0)
    all_counts = lax.all_gather(counts[None, :], "expert", axis=0, tiled=True)
    my_expert = lax.axis_index("expert") // 2
    chosen = jnp.arange(experts, dtype=jnp.int32)[None, :] == my_expert
    my_counts = jnp.sum(jnp.where(chosen, all_counts, 0), axis=1)
    valid = (jnp.arange(capacity, dtype=jnp.int32)[None, :] < my_counts[:, None]).reshape(-1)
    inputs_flat = expert_inputs.reshape(slot_rows, width)
    grad_flat = hidden_grad.reshape(slot_rows, -1)
    masked = jnp.where(valid[:, None], grad_flat, jnp.zeros_like(grad_flat))

    wbf = weight.astype(jnp.bfloat16)
    partner = lax.ppermute(wbf, "core", SWAP)
    chip_w = jnp.where(
        me_c == 0, jnp.concatenate([wbf, partner], axis=0), jnp.concatenate([partner, wbf], axis=0)
    )
    by_class = inputs_flat.reshape(slot_rows, n_z, CORES, rows)
    in_mine = lax.dynamic_index_in_dim(by_class, me_c, axis=2, keepdims=False)
    in_other = lax.dynamic_index_in_dim(by_class, 1 - me_c, axis=2, keepdims=False)
    dims = (((0,), (0,)), ((), ()))
    g_other = lax.dot_general(
        in_other.reshape(slot_rows, n_z * rows), masked, dims, preferred_element_type=jnp.float32
    )
    g_recv = lax.ppermute(g_other.astype(jnp.bfloat16), "core", SWAP)
    g_mine = lax.dot_general(
        in_mine.reshape(slot_rows, n_z * rows), masked, dims, preferred_element_type=jnp.float32
    )
    chip = (g_mine + g_recv.astype(jnp.float32)).astype(jnp.bfloat16)
    held = []
    cur = chip_w
    owned = None
    for t in range(1, n_z):
        if t == n_z - 1 or n_z == 2:
            cur, chip = lax.optimization_barrier((cur, chip))
            owned = lax.psum_scatter(chip, "z", scatter_dimension=0, tiled=True)
        cur = lax.ppermute(cur, DP, flood_pairs(n_z, t))
        held.append(cur)
    held = lax.optimization_barrier(tuple(held))
    other_held = lax.ppermute(held, "core", SWAP)
    cols = (((1,), (1,)), ((), ()))
    own_rows = lax.dot_general(masked, chip_w, cols, preferred_element_type=jnp.float32)
    recv_own = lax.all_to_all(
        own_rows.reshape(n_expert, capacity, CORES * rows), "expert", 0, 0, tiled=True
    )
    parts = []
    for r in range(1, n_z):
        up = jnp.where(me_c == 0, other_held[r - 1], held[r - 1])
        down = jnp.where(me_c == 0, held[n_z - r - 1], other_held[n_z - r - 1])
        parts.append(jnp.where(me_z + r < n_z, up, down))
    w_rest = jnp.concatenate(parts, axis=0)
    rest_rows = lax.dot_general(masked, w_rest, cols, preferred_element_type=jnp.float32)
    recv_rest = lax.all_to_all(
        rest_rows.reshape(n_expert, capacity, width - CORES * rows), "expert", 0, 0, tiled=True
    )
    received = jnp.concatenate([recv_own, recv_rest], axis=2)
    paired = jnp.sum(received.reshape(experts, 2, capacity, width), axis=1).astype(jnp.bfloat16)
    target = (routes * capacity + slots).reshape(tok_count, top_count, 1)
    choose = jnp.sum(
        (target == jnp.arange(experts * capacity, dtype=jnp.int32)).astype(jnp.int32), axis=1
    ).astype(jnp.bfloat16)
    token_rel = jnp.dot(
        choose, paired.reshape(experts * capacity, width), preferred_element_type=jnp.float32
    ).astype(jnp.bfloat16)
    token_grad = jnp.roll(token_rel.reshape(tok_count, n_z, CORES * rows), me_z, axis=1)
    token_grad = token_grad.reshape(tok_count, width)

    token_grad, owned = lax.optimization_barrier((token_grad, owned))
    owned = owned.astype(jnp.float32)
    new_weight, new_first, new_second = adamw(weight, moment_one, moment_two, owned / loss_scale)
    return (token_grad, new_weight, new_first, new_second)


def solution(mesh):
    n_expert, n_dp = mesh.devices.shape
    split_mesh = Mesh(mesh.devices.reshape(n_expert, n_dp // CORES, CORES), ("expert",) + DP)
    in_specs = (
        P(("expert",) + DP, None),
        P(DP, "expert", None, None),
        P(DP, "expert", None, None),
        P(DP, "expert"),
        P(DP, "expert"),
        P(DP, "expert"),
    )
    out_specs = (P(("expert",) + DP, None), P(DP, "expert"), P(DP, "expert"), P(DP, "expert"))
    return jax.shard_map(
        shards, mesh=split_mesh, in_specs=in_specs, out_specs=out_specs, check_vma=False
    )
```

```python
import jax
import jax.numpy as jnp
from jax import lax
from jax.sharding import Mesh
from jax.sharding import PartitionSpec as P

beta_one = 0.9
beta_two = 0.95
learn_rate = 0.003
decay = 0.1
epsilon = 1e-08
loss_scale = 64.0
bias_one = 1.0 - (0.9**50) ** 2
bias_two = 1.0 - (0.95**50) ** 2
CORES = 2
DP = ("z", "core")


def adamw(weight, moment_one, moment_two, grad):
    new_first = beta_one * moment_one + (1.0 - beta_one) * grad
    new_second = beta_two * moment_two + (1.0 - beta_two) * grad * grad
    update = new_first * (1.0 / bias_one) / (jnp.sqrt(new_second * (1.0 / bias_two)) + epsilon)
    new_weight = weight - learn_rate * (update + decay * weight)
    return (new_weight, new_first, new_second)


SWAP = [(0, 1), (1, 0)]


def flood_pairs(n_z, t):
    up = [(z * CORES, (z + 1) * CORES) for z in range(t - 1, n_z - 1)]
    down = [(z * CORES + 1, (z - 1) * CORES + 1) for z in range(1, n_z - t + 1)]
    return up + down


def shards(routes, expert_inputs, hidden_grad, weight, moment_one, moment_two):
    n_expert = lax.axis_size("expert")
    n_z = lax.axis_size("z")
    experts = n_expert // 2
    slot_rows = expert_inputs.shape[2]
    capacity = slot_rows // n_expert
    width = expert_inputs.shape[3]
    rows = weight.shape[0]
    tok_count = routes.shape[0]
    top_count = routes.shape[1]
    me_c = lax.axis_index("core")
    me_z = lax.axis_index("z")
    flat_routes = routes.reshape(-1)
    onehot = (flat_routes[:, None] == jnp.arange(experts, dtype=jnp.int32)[None, :]).astype(
        jnp.int32
    )
    running = jnp.cumsum(onehot, axis=0)
    slots = jnp.sum((running - 1) * onehot, axis=1).reshape(tok_count, top_count)
    counts = jnp.sum(onehot, axis=0)
    all_counts = lax.all_gather(counts[None, :], "expert", axis=0, tiled=True)
    my_expert = lax.axis_index("expert") // 2
    chosen = jnp.arange(experts, dtype=jnp.int32)[None, :] == my_expert
    my_counts = jnp.sum(jnp.where(chosen, all_counts, 0), axis=1)
    valid = (jnp.arange(capacity, dtype=jnp.int32)[None, :] < my_counts[:, None]).reshape(-1)
    inputs_flat = expert_inputs.reshape(slot_rows, width)
    grad_flat = hidden_grad.reshape(slot_rows, -1)
    masked = jnp.where(valid[:, None], grad_flat, jnp.zeros_like(grad_flat))

    wbf = weight.astype(jnp.bfloat16)
    partner = lax.ppermute(wbf, "core", SWAP)
    chip_w = jnp.where(
        me_c == 0, jnp.concatenate([wbf, partner], axis=0), jnp.concatenate([partner, wbf], axis=0)
    )
    held = []
    cur = chip_w
    for t in range(1, n_z):
        cur = lax.ppermute(cur, DP, flood_pairs(n_z, t))
        held.append(cur)
    by_class = inputs_flat.reshape(slot_rows, n_z, CORES, rows)
    in_mine = lax.dynamic_index_in_dim(by_class, me_c, axis=2, keepdims=False)
    in_other = lax.dynamic_index_in_dim(by_class, 1 - me_c, axis=2, keepdims=False)
    dims = (((0,), (0,)), ((), ()))
    g_other = lax.dot_general(
        in_other.reshape(slot_rows, n_z * rows), masked, dims, preferred_element_type=jnp.float32
    )
    g_recv = lax.ppermute(g_other.astype(jnp.bfloat16), "core", SWAP)
    g_mine = lax.dot_general(
        in_mine.reshape(slot_rows, n_z * rows), masked, dims, preferred_element_type=jnp.float32
    )
    chip = (g_mine + g_recv.astype(jnp.float32)).astype(jnp.bfloat16)
    held, chip = lax.optimization_barrier((tuple(held), chip))
    owned = lax.psum_scatter(chip, "z", scatter_dimension=0, tiled=True)
    other_held = lax.ppermute(held, "core", SWAP)
    cols = (((1,), (1,)), ((), ()))
    own_rows = lax.dot_general(masked, chip_w, cols, preferred_element_type=jnp.float32)
    recv_own = lax.all_to_all(
        own_rows.reshape(n_expert, capacity, CORES * rows), "expert", 0, 0, tiled=True
    )
    parts = []
    for r in range(1, n_z):
        up = jnp.where(me_c == 0, other_held[r - 1], held[r - 1])
        down = jnp.where(me_c == 0, held[n_z - r - 1], other_held[n_z - r - 1])
        parts.append(jnp.where(me_z + r < n_z, up, down))
    w_rest = jnp.concatenate(parts, axis=0)
    rest_rows = lax.dot_general(masked, w_rest, cols, preferred_element_type=jnp.float32)
    recv_rest = lax.all_to_all(
        rest_rows.reshape(n_expert, capacity, width - CORES * rows), "expert", 0, 0, tiled=True
    )
    received = jnp.concatenate([recv_own, recv_rest], axis=2)
    paired = jnp.sum(received.reshape(experts, 2, capacity, width), axis=1).astype(jnp.bfloat16)
    target = (routes * capacity + slots).reshape(tok_count, top_count, 1)
    choose = jnp.sum(
        (target == jnp.arange(experts * capacity, dtype=jnp.int32)).astype(jnp.int32), axis=1
    ).astype(jnp.bfloat16)
    token_rel = jnp.dot(
        choose, paired.reshape(experts * capacity, width), preferred_element_type=jnp.float32
    ).astype(jnp.bfloat16)
    token_grad = jnp.roll(token_rel.reshape(tok_count, n_z, CORES * rows), me_z, axis=1)
    token_grad = token_grad.reshape(tok_count, width)

    token_grad, owned = lax.optimization_barrier((token_grad, owned))
    owned = owned.astype(jnp.float32)
    new_weight, new_first, new_second = adamw(weight, moment_one, moment_two, owned / loss_scale)
    return (token_grad, new_weight, new_first, new_second)


def solution(mesh):
    n_expert, n_dp = mesh.devices.shape
    split_mesh = Mesh(mesh.devices.reshape(n_expert, n_dp // CORES, CORES), ("expert",) + DP)
    in_specs = (
        P(("expert",) + DP, None),
        P(DP, "expert", None, None),
        P(DP, "expert", None, None),
        P(DP, "expert"),
        P(DP, "expert"),
        P(DP, "expert"),
    )
    out_specs = (P(("expert",) + DP, None), P(DP, "expert"), P(DP, "expert"), P(DP, "expert"))
    return jax.shard_map(
        shards, mesh=split_mesh, in_specs=in_specs, out_specs=out_specs, check_vma=False
    )
```

```python
import jax
import jax.numpy as jnp
from jax import lax
from jax.sharding import Mesh
from jax.sharding import PartitionSpec as P

beta_one = 0.9
beta_two = 0.95
learn_rate = 0.003
decay = 0.1
epsilon = 1e-08
loss_scale = 64.0
bias_one = 1.0 - (0.9**50) ** 2
bias_two = 1.0 - (0.95**50) ** 2
CORES = 2
DP = ("z", "core")


def adamw(weight, moment_one, moment_two, grad):
    new_first = beta_one * moment_one + (1.0 - beta_one) * grad
    new_second = beta_two * moment_two + (1.0 - beta_two) * grad * grad
    update = new_first / bias_one / (jnp.sqrt(new_second / bias_two) + epsilon)
    new_weight = weight - learn_rate * (update + decay * weight)
    return (new_weight, new_first, new_second)


SWAP = [(0, 1), (1, 0)]


def flood_pairs(n_z, t):
    up = [(z * CORES, (z + 1) * CORES) for z in range(t - 1, n_z - 1)]
    down = [(z * CORES + 1, (z - 1) * CORES + 1) for z in range(1, n_z - t + 1)]
    return up + down


def shards(routes, expert_inputs, hidden_grad, weight, moment_one, moment_two):
    n_expert = lax.axis_size("expert")
    n_z = lax.axis_size("z")
    experts = n_expert // 2
    slot_rows = expert_inputs.shape[2]
    capacity = slot_rows // n_expert
    width = expert_inputs.shape[3]
    rows = weight.shape[0]
    tok_count = routes.shape[0]
    top_count = routes.shape[1]
    me_c = lax.axis_index("core")
    me_z = lax.axis_index("z")
    flat_routes = routes.reshape(-1)
    onehot = (flat_routes[:, None] == jnp.arange(experts, dtype=jnp.int32)[None, :]).astype(
        jnp.int32
    )
    running = jnp.cumsum(onehot, axis=0)
    slots = jnp.sum((running - 1) * onehot, axis=1).reshape(tok_count, top_count)
    counts = jnp.sum(onehot, axis=0)
    all_counts = lax.all_gather(counts[None, :], "expert", axis=0, tiled=True)
    my_expert = lax.axis_index("expert") // 2
    chosen = jnp.arange(experts, dtype=jnp.int32)[None, :] == my_expert
    my_counts = jnp.sum(jnp.where(chosen, all_counts, 0), axis=1)
    valid = (jnp.arange(capacity, dtype=jnp.int32)[None, :] < my_counts[:, None]).reshape(-1)
    inputs_flat = expert_inputs.reshape(slot_rows, width)
    grad_flat = hidden_grad.reshape(slot_rows, -1)
    masked = jnp.where(valid[:, None], grad_flat, jnp.zeros_like(grad_flat))

    wbf = weight.astype(jnp.bfloat16)
    partner = lax.ppermute(wbf, "core", SWAP)
    chip_w = jnp.concatenate([wbf, partner], axis=0)
    held = []
    cur = chip_w
    for t in range(1, n_z):
        cur = lax.ppermute(cur, DP, flood_pairs(n_z, t))
        held.append(cur)
    by_class = inputs_flat.reshape(slot_rows, n_z, CORES, rows)
    in_mine = lax.dynamic_index_in_dim(by_class, me_c, axis=2, keepdims=False)
    in_other = lax.dynamic_index_in_dim(by_class, 1 - me_c, axis=2, keepdims=False)
    dims = (((0,), (0,)), ((), ()))
    g_other = lax.dot_general(
        in_other.reshape(slot_rows, n_z * rows), masked, dims, preferred_element_type=jnp.float32
    )
    g_recv = lax.ppermute(g_other.astype(jnp.bfloat16), "core", SWAP)
    g_mine = lax.dot_general(
        in_mine.reshape(slot_rows, n_z * rows), masked, dims, preferred_element_type=jnp.float32
    )
    chip = (g_mine + g_recv.astype(jnp.float32)).astype(jnp.bfloat16)
    held, chip = lax.optimization_barrier((tuple(held), chip))
    owned = lax.psum_scatter(chip, "z", scatter_dimension=0, tiled=True)
    other_held = lax.ppermute(held, "core", SWAP)
    cols = (((1,), (1,)), ((), ()))
    own_rows = lax.dot_general(masked, chip_w, cols, preferred_element_type=jnp.float32)
    recv_own = lax.all_to_all(
        own_rows.reshape(n_expert, capacity, CORES * rows), "expert", 0, 0, tiled=True
    )
    parts = []
    for r in range(1, n_z):
        up = jnp.where(me_c == 0, other_held[r - 1], held[r - 1])
        down = jnp.where(me_c == 0, held[n_z - r - 1], other_held[n_z - r - 1])
        parts.append(jnp.where(me_z + r < n_z, up, down))
    w_rest = jnp.concatenate(parts, axis=0)
    rest_rows = lax.dot_general(masked, w_rest, cols, preferred_element_type=jnp.float32)
    recv_rest = lax.all_to_all(
        rest_rows.reshape(n_expert, capacity, width - CORES * rows), "expert", 0, 0, tiled=True
    )
    received = jnp.concatenate([recv_own, recv_rest], axis=2)
    paired = jnp.sum(received.reshape(experts, 2, capacity, width), axis=1).astype(jnp.bfloat16)
    target = (routes * capacity + slots).reshape(tok_count, top_count, 1)
    choose = jnp.sum(
        (target == jnp.arange(experts * capacity, dtype=jnp.int32)).astype(jnp.int32), axis=1
    ).astype(jnp.bfloat16)
    token_rel = jnp.dot(
        choose, paired.reshape(experts * capacity, width), preferred_element_type=jnp.float32
    ).astype(jnp.bfloat16)
    split = token_rel.reshape(tok_count, n_z, CORES, rows)
    swapped = jnp.concatenate(
        [(me_c == 1)[None], me_z + jnp.arange(1, n_z, dtype=jnp.int32) < n_z]
    )
    split = jnp.where(swapped[None, :, None, None], split[:, :, ::-1], split)
    token_grad = jnp.roll(split.reshape(tok_count, n_z, CORES * rows), me_z, axis=1)
    token_grad = token_grad.reshape(tok_count, width)

    token_grad, owned = lax.optimization_barrier((token_grad, owned))
    owned = owned.astype(jnp.float32)
    new_weight, new_first, new_second = adamw(weight, moment_one, moment_two, owned / loss_scale)
    return (token_grad, new_weight, new_first, new_second)


def solution(mesh):
    n_expert, n_dp = mesh.devices.shape
    split_mesh = Mesh(mesh.devices.reshape(n_expert, n_dp // CORES, CORES), ("expert",) + DP)
    in_specs = (
        P(("expert",) + DP, None),
        P(DP, "expert", None, None),
        P(DP, "expert", None, None),
        P(DP, "expert"),
        P(DP, "expert"),
        P(DP, "expert"),
    )
    out_specs = (P(("expert",) + DP, None), P(DP, "expert"), P(DP, "expert"), P(DP, "expert"))
    return jax.shard_map(
        shards, mesh=split_mesh, in_specs=in_specs, out_specs=out_specs, check_vma=False
    )
```
